256 devices in a mesh: dp: 32 (over x, z_hi, y), owner: 8 (over z_lo, core).
Axes of the slice: x: 4, y: 4, z: 8 (z_hi: 2, z_lo: 4; z = z_hi * 4 + z_lo), core: 2. Of those that a mesh axis runs over, the one named last changes fastest.
Arguments:
- line_columns: bfloat16 [8, 131072, 512], P(None, ('dp', 'owner')), may hold values from -12 to 12
- line_widths: int32 [256, 4], P(('dp', 'owner')), may hold values from 1 to 128, as said below
- layer_owner: int32 [8], replicated, may hold values from 0 to 7, each once
Outputs:
- preconditioned: float32 [8, 1152, 128], replicated
The draws below stay inside these ranges and needn't reach their ends.
Inputs may be any that keep to these rules, and one draw needn't show every extreme that they name: `line_widths`: row b holds the widths of the 4 lines of device b, laid end to end from its first position; in every draw the lines of some device all have width 128.
All inputs are finite; a program needn't handle non-finite values.
Results may differ from the reference program's by a relative error of at most 0.0003.
Values may be sent and summed in bfloat16 or wider, within the bound.
No kernel may reach another device: no remote copies, remote signals or barrier semaphores. Data moves between devices by JAX's collectives and lax.ppermute only.
A program may use at most 128 MiB of HBM per device.

```python
import math
import jax
import jax.numpy as jnp
from jax import lax

C = 128
WMAX = 128
LINES_DEV = 4
POS_DEV = 512
ROWS = 131072
LAYERS = 8
DEVICES = 256


filter_ratio = 0.88


filter_taps = 16


def filter_norm():
    total = 0.0
    for tap in range(filter_taps):
        total = total + filter_ratio ** (2 * tap)
    return 1.0 / math.sqrt(total)


def draw_line_columns(key, part):
    layer_key = jax.random.fold_in(key, 11)
    channel_norm = filter_norm()

    def one_layer(layer_index):
        keys = jax.random.split(jax.random.fold_in(layer_key, layer_index), 12)
        source = jax.random.normal(keys[0], (ROWS + 1, 3 * C), jnp.float32)
        row_spread = 0.6
        temporal = source[1:] + 0.6 * source[:-1]
        features = jnp.zeros_like(temporal)
        for tap in range(filter_taps):
            features = features + filter_ratio ** tap * jnp.roll(temporal, tap, axis=1)
        features = features * channel_norm
        column_scale = jnp.exp(jax.random.uniform(keys[1], (1, 3 * C), jnp.float32, -0.8, 0.8))
        row_noise = jax.random.uniform(keys[2], (DEVICES, POS_DEV, 1), jnp.float32, -row_spread, row_spread)
        device_noise = jax.random.uniform(keys[3], (DEVICES, 1, 1), jnp.float32, -0.45, 0.45)
        rising = 0.55 * jnp.arange(DEVICES, dtype=jnp.float32)[:, None, None] / max(DEVICES - 1, 1) - 0.3
        row_scale = jnp.exp(row_noise + device_noise + rising).reshape(ROWS, 1)
        features = features * column_scale * row_scale
        mixing = jax.random.uniform(keys[4], (DEVICES, 1, 1), jnp.float32, -1.5, 1.5)
        mixing = jnp.broadcast_to(mixing, (DEVICES, POS_DEV, 1)).reshape(ROWS, 1)
        gradients = 0.7 * jax.random.normal(keys[5], (ROWS, C), jnp.float32) * row_scale
        for tap_index, shift_size in ((0, 0), (1, 5), (2, 11)):
            base_coef = jax.random.uniform(keys[6 + tap_index], (1, C), jnp.float32, -0.8, 0.8)
            varying = jax.random.uniform(keys[9 + tap_index], (1, C), jnp.float32, -0.8, 0.8)
            channel_part = features[:, tap_index * C:(tap_index + 1) * C]
            gradients = gradients + (base_coef + mixing * varying) * jnp.roll(channel_part, shift_size, axis=1)
        values = jnp.concatenate([features, gradients], axis=1)
        return jnp.clip(values, -12.0, 12.0).astype(jnp.bfloat16)
    return lax.map(one_layer, jnp.arange(LAYERS, dtype=jnp.int32))


def draw_line_widths(key, part):
    keys = jax.random.split(jax.random.fold_in(key, 23), 3)
    bucket_top = jax.random.randint(keys[0], (), WMAX // 4, WMAX + 1, jnp.int32)
    raw_widths = jax.random.randint(keys[1], (DEVICES, LINES_DEV), 0, WMAX, jnp.int32)
    widths = 1 + raw_widths % bucket_top
    full_row = jax.random.randint(keys[2], (), 0, DEVICES, jnp.int32)
    device_rows = jnp.arange(DEVICES, dtype=jnp.int32)[:, None]
    return jnp.where(device_rows == full_row, WMAX, widths).astype(jnp.int32)


def setup_inputs(seed: int = 0) -> dict:
    key_list = jax.random.split(jax.random.key(seed), 4)
    line_columns = draw_line_columns(jax.random.fold_in(key_list[3], 71), 0)
    line_widths = draw_line_widths(jax.random.fold_in(key_list[3], 71), 0)
    layer_owner = jax.random.permutation(key_list[2], LAYERS).astype(jnp.int32)
    return {"line_columns": line_columns, "line_widths": line_widths, "layer_owner": layer_owner}


damping = 0.1

def patch_columns(block, widths):
    positions = block.shape[-2]
    channels = block.shape[-1] // 4
    line_ends = jnp.cumsum(widths, axis=-1).astype(jnp.int32)
    line_starts = line_ends - widths
    place = jnp.arange(positions, dtype=jnp.int32)[:, None]
    opening = jnp.any(place == line_starts[..., None, :], axis=-1)[..., None]
    closing = jnp.any(place + 1 == line_ends[..., None, :], axis=-1)[..., None]
    inside = place < line_ends[..., None, -1:]
    features = block[..., :3 * channels]
    gradients = block[..., 3 * channels:]
    padding = jnp.zeros_like(features[..., :1, :])
    before = jnp.concatenate([padding, features[..., :-1, :]], axis=-2)
    after = jnp.concatenate([features[..., 1:, :], padding], axis=-2)
    before = jnp.where(opening, jnp.zeros_like(before), before)
    after = jnp.where(closing, jnp.zeros_like(after), after)
    stacked = jnp.concatenate([before, features, after, gradients], axis=-1)
    return jnp.where(inside, stacked, jnp.zeros_like(stacked))

def precondition(factor, total_rows):
    full_width = factor.shape[0]
    patch_width = full_width // 10 * 9
    scaled = factor / total_rows
    act_factor = scaled[:patch_width, :patch_width] + damping * jnp.eye(patch_width, dtype=factor.dtype)
    grad_factor = scaled[patch_width:, patch_width:] + damping * jnp.eye(full_width - patch_width, dtype=factor.dtype)
    cross_term = scaled[:patch_width, patch_width:]
    act_cholesky = jnp.linalg.cholesky(act_factor)
    left_solved = jax.scipy.linalg.cho_solve((act_cholesky, True), cross_term)
    grad_cholesky = jnp.linalg.cholesky(grad_factor)
    return jax.scipy.linalg.cho_solve((grad_cholesky, True), left_solved.T).T

def reference(line_columns, line_widths, layer_owner):
    results = []
    for slot in range(LAYERS):
        layer_block = lax.dynamic_index_in_dim(line_columns, layer_owner[slot], 0, keepdims=False)
        layer_block = layer_block.reshape(DEVICES, POS_DEV, 4 * C)

        def add_block(running, pieces):
            columns = patch_columns(pieces[0], pieces[1])
            return (running + jnp.dot(columns.T.astype(jnp.float32), columns.astype(jnp.float32), preferred_element_type=jnp.float32), None)
        factor, _ = lax.scan(add_block, jnp.zeros((10 * C, 10 * C), jnp.float32), (layer_block, line_widths))
        results.append(precondition(factor, ROWS))
    return jnp.stack(results)
```

```python
import numpy as np
import jax
import jax.numpy as jnp
from jax import lax
from jax.sharding import PartitionSpec as P

damping = 0.1


def patch_columns(block, widths):
    positions = block.shape[-2]
    channels = block.shape[-1] // 4
    line_ends = jnp.cumsum(widths, axis=-1).astype(jnp.int32)
    line_starts = line_ends - widths
    place = jnp.arange(positions, dtype=jnp.int32)[:, None]
    opening = jnp.any(place == line_starts[..., None, :], axis=-1)[..., None]
    closing = jnp.any(place + 1 == line_ends[..., None, :], axis=-1)[..., None]
    inside = place < line_ends[..., None, -1:]
    features = block[..., : 3 * channels]
    gradients = block[..., 3 * channels :]
    padding = jnp.zeros_like(features[..., :1, :])
    before = jnp.concatenate([padding, features[..., :-1, :]], axis=-2)
    after = jnp.concatenate([features[..., 1:, :], padding], axis=-2)
    before = jnp.where(opening, jnp.zeros_like(before), before)
    after = jnp.where(closing, jnp.zeros_like(after), after)
    stacked = jnp.concatenate([before, features, after, gradients], axis=-1)
    return jnp.where(inside, stacked, jnp.zeros_like(stacked))


def precondition(factor, total_rows):
    full_width = factor.shape[0]
    patch_width = full_width // 10 * 9
    scaled = factor / total_rows
    act_factor = scaled[:patch_width, :patch_width] + damping * jnp.eye(
        patch_width, dtype=factor.dtype
    )
    grad_factor = scaled[patch_width:, patch_width:] + damping * jnp.eye(
        full_width - patch_width, dtype=factor.dtype
    )
    cross_term = scaled[:patch_width, patch_width:]
    act_cholesky = jnp.linalg.cholesky(act_factor)
    left_solved = jax.scipy.linalg.cho_solve((act_cholesky, True), cross_term)
    grad_cholesky = jnp.linalg.cholesky(grad_factor)
    return jax.scipy.linalg.cho_solve((grad_cholesky, True), left_solved.T).T


def _tri_pairs(nb):
    return [(i, j) for i in range(nb) for j in range(i + 1)]


def pack_lower(gram, block):
    nb = gram.shape[0] // block
    tiles = gram.reshape(nb, block, nb, block).transpose(0, 2, 1, 3)
    pairs = _tri_pairs(nb)
    rows = np.array([p[0] for p in pairs], dtype=np.int32)
    cols = np.array([p[1] for p in pairs], dtype=np.int32)
    return tiles[rows, cols]


def unpack_lower(blocks, nb):
    block = blocks.shape[-1]
    index = {p: k for k, p in enumerate(_tri_pairs(nb))}
    pick = np.array([[index[(max(i, j), min(i, j))] for j in range(nb)] for i in range(nb)], dtype=np.int32)
    upper = np.array([[i < j for j in range(nb)] for i in range(nb)])
    tiles = blocks[pick]
    tiles = jnp.where(upper[:, :, None, None], jnp.swapaxes(tiles, -1, -2), tiles)
    return tiles.transpose(0, 2, 1, 3).reshape(nb * block, nb * block)


def body(line_columns, line_widths, layer_owner):
    layer_count, positions, packed_width = line_columns.shape
    channels = packed_width // 4
    full_width = 10 * channels
    n_replicas = lax.axis_size("dp")
    n_owners = lax.axis_size("owner")
    per_owner = layer_count // n_owners
    total_rows = n_replicas * n_owners * positions
    ordered = jnp.take(line_columns, layer_owner, axis=0)
    width_copies = jnp.broadcast_to(line_widths[None, :, :], (n_owners, 1, line_widths.shape[1]))
    received, source_widths = (
        lax.all_to_all(ordered, "owner", split_axis=0, concat_axis=1, tiled=True),
        lax.all_to_all(width_copies, "owner", split_axis=0, concat_axis=1, tiled=True),
    )
    blocks = received.reshape(per_owner, n_owners, positions, packed_width)
    columns = patch_columns(blocks, source_widths.reshape(n_owners, line_widths.shape[1]))
    columns = columns.reshape(n_owners * positions, full_width)
    gram = jnp.dot(columns.T, columns, preferred_element_type=jnp.float32)
    block = 128
    nb = full_width // block
    packed = pack_lower(gram, block)
    n_blocks = packed.shape[0]
    padded = -(-n_blocks * block // (8 * n_replicas)) * 8 * n_replicas // block
    packed = jnp.concatenate(
        [packed, jnp.zeros((padded - n_blocks, block, block), packed.dtype)], axis=0
    )
    chunk = padded * block // n_replicas
    packed = packed.reshape(n_replicas, chunk, block)
    mine = lax.psum_scatter(packed, "dp", scatter_dimension=0, tiled=True)
    gathered = lax.all_gather(mine, "dp", axis=0, tiled=True)
    gathered = gathered.reshape(padded, block, block)[:n_blocks]
    factor = unpack_lower(gathered, nb)
    results = precondition(factor, total_rows)[None]
    return lax.all_gather(results, "owner", axis=0, tiled=True)


def solution(mesh):
    in_specs = (P(None, ("dp", "owner"), None), P(("dp", "owner"), None), P())
    out_specs = P()
    return jax.shard_map(body, mesh=mesh, in_specs=in_specs, out_specs=out_specs, check_vma=False)
```

```python
import numpy as np
import jax
import jax.numpy as jnp
from jax import lax
from jax.sharding import PartitionSpec as P

damping = 0.1


def patch_columns(block, widths):
    positions = block.shape[-2]
    channels = block.shape[-1] // 4
    line_ends = jnp.cumsum(widths, axis=-1).astype(jnp.int32)
    line_starts = line_ends - widths
    place = jnp.arange(positions, dtype=jnp.int32)[:, None]
    opening = jnp.any(place == line_starts[..., None, :], axis=-1)[..., None]
    closing = jnp.any(place + 1 == line_ends[..., None, :], axis=-1)[..., None]
    inside = place < line_ends[..., None, -1:]
    features = block[..., : 3 * channels]
    gradients = block[..., 3 * channels :]
    padding = jnp.zeros_like(features[..., :1, :])
    before = jnp.concatenate([padding, features[..., :-1, :]], axis=-2)
    after = jnp.concatenate([features[..., 1:, :], padding], axis=-2)
    before = jnp.where(opening, jnp.zeros_like(before), before)
    after = jnp.where(closing, jnp.zeros_like(after), after)
    stacked = jnp.concatenate([before, features, after, gradients], axis=-1)
    return jnp.where(inside, stacked, jnp.zeros_like(stacked))


def precondition(factor, total_rows):
    full_width = factor.shape[0]
    patch_width = full_width // 10 * 9
    scaled = factor / total_rows
    act_factor = scaled[:patch_width, :patch_width] + damping * jnp.eye(
        patch_width, dtype=factor.dtype
    )
    grad_factor = scaled[patch_width:, patch_width:] + damping * jnp.eye(
        full_width - patch_width, dtype=factor.dtype
    )
    cross_term = scaled[:patch_width, patch_width:]
    act_cholesky = jnp.linalg.cholesky(act_factor)
    left_solved = jax.scipy.linalg.cho_solve((act_cholesky, True), cross_term)
    grad_cholesky = jnp.linalg.cholesky(grad_factor)
    return jax.scipy.linalg.cho_solve((grad_cholesky, True), left_solved.T).T


def _tri_pairs(nb):
    return [(i, j) for i in range(nb) for j in range(i + 1)]


def pack_lower(gram, block):
    nb = gram.shape[0] // block
    tiles = gram.reshape(nb, block, nb, block).transpose(0, 2, 1, 3)
    pairs = _tri_pairs(nb)
    rows = np.array([p[0] for p in pairs], dtype=np.int32)
    cols = np.array([p[1] for p in pairs], dtype=np.int32)
    return tiles[rows, cols]


def unpack_lower(blocks, nb):
    block = blocks.shape[-1]
    index = {p: k for k, p in enumerate(_tri_pairs(nb))}
    pick = np.array([[index[(max(i, j), min(i, j))] for j in range(nb)] for i in range(nb)], dtype=np.int32)
    upper = np.array([[i < j for j in range(nb)] for i in range(nb)])
    tiles = blocks[pick]
    tiles = jnp.where(upper[:, :, None, None], jnp.swapaxes(tiles, -1, -2), tiles)
    return tiles.transpose(0, 2, 1, 3).reshape(nb * block, nb * block)


def body(line_columns, line_widths, layer_owner):
    layer_count, positions, packed_width = line_columns.shape
    channels = packed_width // 4
    full_width = 10 * channels
    n_replicas = 1
    for axis in DP_AXES:
        n_replicas = n_replicas * lax.axis_size(axis)
    n_owners = lax.axis_size("owner")
    per_owner = layer_count // n_owners
    total_rows = n_replicas * n_owners * positions
    ordered = jnp.take(line_columns, layer_owner, axis=0)
    width_copies = jnp.broadcast_to(line_widths[None, :, :], (n_owners, 1, line_widths.shape[1]))
    received, source_widths = (
        lax.all_to_all(ordered, "owner", split_axis=0, concat_axis=1, tiled=True),
        lax.all_to_all(width_copies, "owner", split_axis=0, concat_axis=1, tiled=True),
    )
    blocks = received.reshape(per_owner, n_owners, positions, packed_width)
    columns = patch_columns(blocks, source_widths.reshape(n_owners, line_widths.shape[1]))
    columns = columns.reshape(n_owners * positions, full_width)
    gram = jnp.dot(columns.T, columns, preferred_element_type=jnp.float32)
    block = 128
    nb = full_width // block
    packed = pack_lower(gram, block)
    n_blocks = packed.shape[0]
    padded = -(-n_blocks * block // (8 * n_replicas)) * 8 * n_replicas // block
    packed = jnp.concatenate(
        [packed, jnp.zeros((padded - n_blocks, block, block), packed.dtype)], axis=0
    )
    chunk = padded * block // n_replicas
    packed = packed.reshape(n_replicas, chunk, block)
    mine = packed.reshape(padded * block, block)
    for axis in DP_AXES[::-1]:
        mine = lax.psum_scatter(mine, axis, scatter_dimension=0, tiled=True)
    gathered = mine
    for axis in DP_AXES:
        gathered = lax.all_gather(gathered, axis, axis=0, tiled=True)
    gathered = gathered.reshape(padded, block, block)[:n_blocks]
    factor = unpack_lower(gathered, nb)
    results = precondition(factor, total_rows)[None]
    return lax.all_gather(results, "owner", axis=0, tiled=True)


DP_AXES = ("dp_x", "dp_z", "dp_y")


def solution(mesh):
    dp_shape = (4, 2, mesh.shape["dp"] // 8)
    devices = mesh.devices.reshape(dp_shape + (mesh.shape["owner"],))
    fine = jax.sharding.Mesh(devices, DP_AXES + ("owner",))
    rows = DP_AXES + ("owner",)
    in_specs = (P(None, rows, None), P(rows, None), P())
    out_specs = P()
    return jax.shard_map(body, mesh=fine, in_specs=in_specs, out_specs=out_specs, check_vma=False)
```

```python
import numpy as np
import jax
import jax.numpy as jnp
from jax import lax
from jax.sharding import PartitionSpec as P

damping = 0.1


def patch_columns(block, widths):
    positions = block.shape[-2]
    channels = block.shape[-1] // 4
    line_ends = jnp.cumsum(widths, axis=-1).astype(jnp.int32)
    line_starts = line_ends - widths
    place = jnp.arange(positions, dtype=jnp.int32)[:, None]
    opening = jnp.any(place == line_starts[..., None, :], axis=-1)[..., None]
    closing = jnp.any(place + 1 == line_ends[..., None, :], axis=-1)[..., None]
    inside = place < line_ends[..., None, -1:]
    features = block[..., : 3 * channels]
    gradients = block[..., 3 * channels :]
    padding = jnp.zeros_like(features[..., :1, :])
    before = jnp.concatenate([padding, features[..., :-1, :]], axis=-2)
    after = jnp.concatenate([features[..., 1:, :], padding], axis=-2)
    before = jnp.where(opening, jnp.zeros_like(before), before)
    after = jnp.where(closing, jnp.zeros_like(after), after)
    stacked = jnp.concatenate([before, features, after, gradients], axis=-1)
    return jnp.where(inside, stacked, jnp.zeros_like(stacked))


def precondition(factor, total_rows):
    full_width = factor.shape[0]
    patch_width = full_width // 10 * 9
    scaled = factor / total_rows
    act_factor = scaled[:patch_width, :patch_width] + damping * jnp.eye(
        patch_width, dtype=factor.dtype
    )
    grad_factor = scaled[patch_width:, patch_width:] + damping * jnp.eye(
        full_width - patch_width, dtype=factor.dtype
    )
    cross_term = scaled[:patch_width, patch_width:]
    act_cholesky = jnp.linalg.cholesky(act_factor)
    left_solved = jax.scipy.linalg.cho_solve((act_cholesky, True), cross_term)
    grad_cholesky = jnp.linalg.cholesky(grad_factor)
    return jax.scipy.linalg.cho_solve((grad_cholesky, True), left_solved.T).T


def _tri_pairs(nb):
    return [(i, j) for i in range(nb) for j in range(i + 1)]


def pack_lower(gram, block):
    nb = gram.shape[0] // block
    tiles = gram.reshape(nb, block, nb, block).transpose(0, 2, 1, 3)
    pairs = _tri_pairs(nb)
    rows = np.array([p[0] for p in pairs], dtype=np.int32)
    cols = np.array([p[1] for p in pairs], dtype=np.int32)
    return tiles[rows, cols]


def unpack_lower(blocks, nb):
    block = blocks.shape[-1]
    index = {p: k for k, p in enumerate(_tri_pairs(nb))}
    pick = np.array([[index[(max(i, j), min(i, j))] for j in range(nb)] for i in range(nb)], dtype=np.int32)
    upper = np.array([[i < j for j in range(nb)] for i in range(nb)])
    tiles = blocks[pick]
    tiles = jnp.where(upper[:, :, None, None], jnp.swapaxes(tiles, -1, -2), tiles)
    return tiles.transpose(0, 2, 1, 3).reshape(nb * block, nb * block)


HIGH = lax.Precision.HIGHEST


def _mm(a, b):
    return jnp.dot(a, b, precision=HIGH, preferred_element_type=jnp.float32)


def _mm_t(a, b):
    return lax.dot_general(a, b, (((0,), (0,)), ((), ())), precision=HIGH,
                           preferred_element_type=jnp.float32)


def _mm_nt(a, b):
    return lax.dot_general(a, b, (((1,), (1,)), ((), ())), precision=HIGH,
                           preferred_element_type=jnp.float32)


def _chol_inv(block):
    lower = jnp.linalg.cholesky(block, symmetrize_input=False)
    eye = jnp.eye(block.shape[0], dtype=block.dtype)
    inverse = lax.linalg.triangular_solve(lower, eye, left_side=True, lower=True)
    return lower, inverse


def precondition_blocks(blocks, nb, total_rows):
    block = blocks.shape[-1]
    na = nb - 1
    index = {p: k for k, p in enumerate(_tri_pairs(nb))}
    zero = len(index)
    pick = np.array([[index[(i, j)] if i >= j else zero for j in range(na)] for i in range(nb)],
                    dtype=np.int32)
    scale = 1.0 / total_rows
    tiles = blocks[pick] * scale
    work = tiles.transpose(0, 2, 1, 3).reshape(nb * block, na * block)
    eye = jnp.eye(block, dtype=blocks.dtype)
    grad_factor = blocks[index[(na, na)]] * scale + damping * eye
    inverses = []
    for k in range(na):
        lo = k * block
        hi = lo + block
        diag = work[lo:hi, lo:hi] + damping * eye
        lower, inverse = _chol_inv(diag)
        inverses.append(inverse)
        panel = _mm_nt(work[hi:, lo:hi], inverse)
        work = work.at[lo:hi, lo:hi].set(lower)
        work = work.at[hi:, lo:hi].set(panel)
        if k + 1 < na:
            update = _mm_nt(panel, panel[: (na - k - 1) * block])
            work = work.at[hi:, hi:].add(-update)
    solved_t = work[na * block:, :]
    pieces = [None] * na
    for k in reversed(range(na)):
        lo = k * block
        hi = lo + block
        rhs = solved_t[:, lo:hi].T
        if k + 1 < na:
            below = jnp.concatenate(pieces[k + 1:], axis=0)
            rhs = rhs - _mm_t(work[hi:na * block, lo:hi], below)
        pieces[k] = _mm_t(inverses[k], rhs)
    left_solved = jnp.concatenate(pieces, axis=0)
    _, grad_inverse = _chol_inv(grad_factor)
    return _mm(_mm_nt(left_solved, grad_inverse), grad_inverse)


def body(line_columns, line_widths, layer_owner):
    layer_count, positions, packed_width = line_columns.shape
    channels = packed_width // 4
    full_width = 10 * channels
    n_replicas = 1
    for axis in DP_AXES:
        n_replicas = n_replicas * lax.axis_size(axis)
    n_owners = lax.axis_size("owner")
    per_owner = layer_count // n_owners
    total_rows = n_replicas * n_owners * positions
    ordered = jnp.take(line_columns, layer_owner, axis=0)
    width_copies = jnp.broadcast_to(line_widths[None, :, :], (n_owners, 1, line_widths.shape[1]))
    received, source_widths = (
        lax.all_to_all(ordered, "owner", split_axis=0, concat_axis=1, tiled=True),
        lax.all_to_all(width_copies, "owner", split_axis=0, concat_axis=1, tiled=True),
    )
    blocks = received.reshape(per_owner, n_owners, positions, packed_width)
    columns = patch_columns(blocks, source_widths.reshape(n_owners, line_widths.shape[1]))
    columns = columns.reshape(n_owners * positions, full_width)
    gram = jnp.dot(columns.T, columns, preferred_element_type=jnp.float32)
    block = 128
    nb = full_width // block
    packed = pack_lower(gram, block)
    n_blocks = packed.shape[0]
    padded = -(-n_blocks * block // (8 * n_replicas)) * 8 * n_replicas // block
    packed = jnp.concatenate(
        [packed, jnp.zeros((padded - n_blocks, block, block), packed.dtype)], axis=0
    )
    chunk = padded * block // n_replicas
    packed = packed.reshape(n_replicas, chunk, block)
    mine = packed.reshape(padded * block, block)
    for axis in DP_AXES[::-1]:
        mine = lax.psum_scatter(mine, axis, scatter_dimension=0, tiled=True)
    gathered = mine
    for axis in DP_AXES:
        gathered = lax.all_gather(gathered, axis, axis=0, tiled=True)
    gathered = gathered.reshape(padded, block, block)
    results = precondition_blocks(gathered, nb, total_rows)[None]
    return lax.all_gather(results, "owner", axis=0, tiled=True)


DP_AXES = ("dp_x", "dp_z", "dp_y")


def solution(mesh):
    dp_shape = (4, 2, mesh.shape["dp"] // 8)
    devices = mesh.devices.reshape(dp_shape + (mesh.shape["owner"],))
    fine = jax.sharding.Mesh(devices, DP_AXES + ("owner",))
    rows = DP_AXES + ("owner",)
    in_specs = (P(None, rows, None), P(rows, None), P())
    out_specs = P()
    return jax.shard_map(body, mesh=fine, in_specs=in_specs, out_specs=out_specs, check_vma=False)
```

```python
import numpy as np
import jax
import jax.numpy as jnp
from jax import lax
from jax.sharding import PartitionSpec as P

damping = 0.1


def patch_columns(block, widths):
    positions = block.shape[-2]
    channels = block.shape[-1] // 4
    line_ends = jnp.cumsum(widths, axis=-1).astype(jnp.int32)
    line_starts = line_ends - widths
    place = jnp.arange(positions, dtype=jnp.int32)[:, None]
    opening = jnp.any(place == line_starts[..., None, :], axis=-1)[..., None]
    closing = jnp.any(place + 1 == line_ends[..., None, :], axis=-1)[..., None]
    inside = place < line_ends[..., None, -1:]
    features = block[..., : 3 * channels]
    gradients = block[..., 3 * channels :]
    padding = jnp.zeros_like(features[..., :1, :])
    before = jnp.concatenate([padding, features[..., :-1, :]], axis=-2)
    after = jnp.concatenate([features[..., 1:, :], padding], axis=-2)
    before = jnp.where(opening, jnp.zeros_like(before), before)
    after = jnp.where(closing, jnp.zeros_like(after), after)
    stacked = jnp.concatenate([before, features, after, gradients], axis=-1)
    return jnp.where(inside, stacked, jnp.zeros_like(stacked))


def precondition(factor, total_rows):
    full_width = factor.shape[0]
    patch_width = full_width // 10 * 9
    scaled = factor / total_rows
    act_factor = scaled[:patch_width, :patch_width] + damping * jnp.eye(
        patch_width, dtype=factor.dtype
    )
    grad_factor = scaled[patch_width:, patch_width:] + damping * jnp.eye(
        full_width - patch_width, dtype=factor.dtype
    )
    cross_term = scaled[:patch_width, patch_width:]
    act_cholesky = jnp.linalg.cholesky(act_factor)
    left_solved = jax.scipy.linalg.cho_solve((act_cholesky, True), cross_term)
    grad_cholesky = jnp.linalg.cholesky(grad_factor)
    return jax.scipy.linalg.cho_solve((grad_cholesky, True), left_solved.T).T


def _tri_pairs(nb):
    return [(i, j) for i in range(nb) for j in range(i + 1)]


def pack_lower(gram, block):
    nb = gram.shape[0] // block
    tiles = gram.reshape(nb, block, nb, block).transpose(0, 2, 1, 3)
    pairs = _tri_pairs(nb)
    rows = np.array([p[0] for p in pairs], dtype=np.int32)
    cols = np.array([p[1] for p in pairs], dtype=np.int32)
    return tiles[rows, cols]


def unpack_lower(blocks, nb):
    block = blocks.shape[-1]
    index = {p: k for k, p in enumerate(_tri_pairs(nb))}
    pick = np.array([[index[(max(i, j), min(i, j))] for j in range(nb)] for i in range(nb)], dtype=np.int32)
    upper = np.array([[i < j for j in range(nb)] for i in range(nb)])
    tiles = blocks[pick]
    tiles = jnp.where(upper[:, :, None, None], jnp.swapaxes(tiles, -1, -2), tiles)
    return tiles.transpose(0, 2, 1, 3).reshape(nb * block, nb * block)


HIGH = lax.Precision.HIGHEST


def _mm(a, b):
    return jnp.dot(a, b, precision=HIGH, preferred_element_type=jnp.float32)


def _mm_t(a, b):
    return lax.dot_general(a, b, (((0,), (0,)), ((), ())), precision=HIGH,
                           preferred_element_type=jnp.float32)


def _mm_nt(a, b):
    return lax.dot_general(a, b, (((1,), (1,)), ((), ())), precision=HIGH,
                           preferred_element_type=jnp.float32)


def _chol_inv(block):
    lower = jnp.linalg.cholesky(block, symmetrize_input=False)
    eye = jnp.eye(block.shape[0], dtype=block.dtype)
    inverse = lax.linalg.triangular_solve(lower, eye, left_side=True, lower=True)
    return lower, inverse


def precondition_blocks(blocks, nb, total_rows):
    block = blocks.shape[-1]
    na = nb - 1
    index = {p: k for k, p in enumerate(_tri_pairs(nb))}
    zero = len(index)
    pick = np.array([[index[(i, j)] if i >= j else zero for j in range(na)] for i in range(nb)],
                    dtype=np.int32)
    scale = 1.0 / total_rows
    tiles = blocks[pick] * scale
    work = tiles.transpose(0, 2, 1, 3).reshape(nb * block, na * block)
    eye = jnp.eye(block, dtype=blocks.dtype)
    grad_factor = blocks[index[(na, na)]] * scale + damping * eye
    inverses = []
    for k in range(na):
        lo = k * block
        hi = lo + block
        diag = work[lo:hi, lo:hi] + damping * eye
        lower, inverse = _chol_inv(diag)
        inverses.append(inverse)
        panel = _mm_nt(work[hi:, lo:hi], inverse)
        work = work.at[lo:hi, lo:hi].set(lower)
        work = work.at[hi:, lo:hi].set(panel)
        if k + 1 < na:
            update = _mm_nt(panel, panel[: (na - k - 1) * block])
            work = work.at[hi:, hi:].add(-update)
    solved_t = work[na * block:, :]
    pieces = [None] * na
    for k in reversed(range(na)):
        lo = k * block
        hi = lo + block
        rhs = solved_t[:, lo:hi].T
        if k + 1 < na:
            below = jnp.concatenate(pieces[k + 1:], axis=0)
            rhs = rhs - _mm_t(work[hi:na * block, lo:hi], below)
        pieces[k] = _mm_t(inverses[k], rhs)
    left_solved = jnp.concatenate(pieces, axis=0)
    _, grad_inverse = _chol_inv(grad_factor)
    return _mm(_mm_nt(left_solved, grad_inverse), grad_inverse)


def body(line_columns, line_widths, layer_owner):
    layer_count, positions, packed_width = line_columns.shape
    channels = packed_width // 4
    full_width = 10 * channels
    n_replicas = 1
    for axis in DP_AXES:
        n_replicas = n_replicas * lax.axis_size(axis)
    n_owners = lax.axis_size("owner")
    per_owner = layer_count // n_owners
    total_rows = n_replicas * n_owners * positions
    ordered = jnp.take(line_columns, layer_owner, axis=0)
    width_copies = jnp.broadcast_to(line_widths[None, :, :], (n_owners, 1, line_widths.shape[1]))
    received, source_widths = (
        lax.all_to_all(ordered, "owner", split_axis=0, concat_axis=1, tiled=True),
        lax.all_to_all(width_copies, "owner", split_axis=0, concat_axis=1, tiled=True),
    )
    blocks = received.reshape(per_owner, n_owners, positions, packed_width)
    columns = patch_columns(blocks, source_widths.reshape(n_owners, line_widths.shape[1]))
    columns = columns.reshape(n_owners * positions, full_width)
    gram = jnp.dot(columns.T, columns, preferred_element_type=jnp.float32)
    block = 128
    nb = full_width // block
    packed = pack_lower(gram, block)
    n_blocks = packed.shape[0]
    padded = -(-n_blocks * block // (8 * n_replicas)) * 8 * n_replicas // block
    packed = jnp.concatenate(
        [packed, jnp.zeros((padded - n_blocks, block, block), packed.dtype)], axis=0
    )
    chunk = padded * block // n_replicas
    packed = packed.reshape(n_replicas, chunk, block)
    mine = packed.reshape(padded * block, block)
    for axis in SCATTER_ORDER:
        mine = lax.psum_scatter(mine, axis, scatter_dimension=0, tiled=True)
    gathered = mine
    for axis in SCATTER_ORDER[::-1]:
        gathered = lax.all_gather(gathered, axis, axis=0, tiled=True)
    gathered = gathered.reshape(padded, block, block)
    results = precondition_blocks(gathered, nb, total_rows)[None]
    return lax.all_gather(results, "owner", axis=0, tiled=True)


DP_AXES = ("dp_x", "dp_z", "dp_y")
SCATTER_ORDER = ("dp_y", "dp_x", "dp_z")


def solution(mesh):
    dp_shape = (4, 2, mesh.shape["dp"] // 8)
    devices = mesh.devices.reshape(dp_shape + (mesh.shape["owner"],))
    fine = jax.sharding.Mesh(devices, DP_AXES + ("owner",))
    rows = DP_AXES + ("owner",)
    in_specs = (P(None, rows, None), P(rows, None), P())
    out_specs = P()
    return jax.shard_map(body, mesh=fine, in_specs=in_specs, out_specs=out_specs, check_vma=False)
```

```python
import numpy as np
import jax
import jax.numpy as jnp
from jax import lax
from jax.experimental import pallas as pl
from jax.experimental.pallas import tpu as pltpu
from jax.sharding import PartitionSpec as P

damping = 0.1


def patch_columns(block, widths):
    positions = block.shape[-2]
    channels = block.shape[-1] // 4
    line_ends = jnp.cumsum(widths, axis=-1).astype(jnp.int32)
    line_starts = line_ends - widths
    place = jnp.arange(positions, dtype=jnp.int32)[:, None]
    opening = jnp.any(place == line_starts[..., None, :], axis=-1)[..., None]
    closing = jnp.any(place + 1 == line_ends[..., None, :], axis=-1)[..., None]
    inside = place < line_ends[..., None, -1:]
    features = block[..., : 3 * channels]
    gradients = block[..., 3 * channels :]
    padding = jnp.zeros_like(features[..., :1, :])
    before = jnp.concatenate([padding, features[..., :-1, :]], axis=-2)
    after = jnp.concatenate([features[..., 1:, :], padding], axis=-2)
    before = jnp.where(opening, jnp.zeros_like(before), before)
    after = jnp.where(closing, jnp.zeros_like(after), after)
    stacked = jnp.concatenate([before, features, after, gradients], axis=-1)
    return jnp.where(inside, stacked, jnp.zeros_like(stacked))


def precondition(factor, total_rows):
    full_width = factor.shape[0]
    patch_width = full_width // 10 * 9
    scaled = factor / total_rows
    act_factor = scaled[:patch_width, :patch_width] + damping * jnp.eye(
        patch_width, dtype=factor.dtype
    )
    grad_factor = scaled[patch_width:, patch_width:] + damping * jnp.eye(
        full_width - patch_width, dtype=factor.dtype
    )
    cross_term = scaled[:patch_width, patch_width:]
    act_cholesky = jnp.linalg.cholesky(act_factor)
    left_solved = jax.scipy.linalg.cho_solve((act_cholesky, True), cross_term)
    grad_cholesky = jnp.linalg.cholesky(grad_factor)
    return jax.scipy.linalg.cho_solve((grad_cholesky, True), left_solved.T).T


def _tri_pairs(nb):
    return [(i, j) for i in range(nb) for j in range(i + 1)]


def pack_lower(gram, block):
    nb = gram.shape[0] // block
    tiles = gram.reshape(nb, block, nb, block).transpose(0, 2, 1, 3)
    pairs = _tri_pairs(nb)
    rows = np.array([p[0] for p in pairs], dtype=np.int32)
    cols = np.array([p[1] for p in pairs], dtype=np.int32)
    return tiles[rows, cols]


def unpack_lower(blocks, nb):
    block = blocks.shape[-1]
    index = {p: k for k, p in enumerate(_tri_pairs(nb))}
    pick = np.array([[index[(max(i, j), min(i, j))] for j in range(nb)] for i in range(nb)], dtype=np.int32)
    upper = np.array([[i < j for j in range(nb)] for i in range(nb)])
    tiles = blocks[pick]
    tiles = jnp.where(upper[:, :, None, None], jnp.swapaxes(tiles, -1, -2), tiles)
    return tiles.transpose(0, 2, 1, 3).reshape(nb * block, nb * block)


HIGH = lax.Precision.HIGHEST


def _mm(a, b):
    return jnp.dot(a, b, precision=HIGH, preferred_element_type=jnp.float32)


def _mm_t(a, b):
    return lax.dot_general(a, b, (((0,), (0,)), ((), ())), precision=HIGH,
                           preferred_element_type=jnp.float32)


def _mm_nt(a, b):
    return lax.dot_general(a, b, (((1,), (1,)), ((), ())), precision=HIGH,
                           preferred_element_type=jnp.float32)


def _chol_inv(block):
    lower = jnp.linalg.cholesky(block, symmetrize_input=False)
    eye = jnp.eye(block.shape[0], dtype=block.dtype)
    inverse = lax.linalg.triangular_solve(lower, eye, left_side=True, lower=True)
    return lower, inverse


def _leaf_kernel(a_ref, w_ref, s_ref):
    n = a_ref.shape[0]
    s_ref[...] = a_ref[...]
    sub = lax.broadcasted_iota(jnp.int32, (n, n), 0)
    lane = lax.broadcasted_iota(jnp.int32, (n, n), 1)
    w_ref[...] = jnp.where(sub == lane, 1.0, 0.0).astype(jnp.float32)
    lane_row = lax.broadcasted_iota(jnp.int32, (1, n), 1)
    sub_col = lax.broadcasted_iota(jnp.int32, (n, 1), 0)

    def step(j, carry):
        a = s_ref[...]
        row = s_ref[pl.ds(j, 1), :]
        pivot = jnp.sum(jnp.where(lane_row == j, row, 0.0), axis=1, keepdims=True)
        inv_root = 1.0 / jnp.sqrt(pivot)
        col = jnp.sum(jnp.where(lane == j, a, 0.0), axis=1, keepdims=True)
        lcol = jnp.where(sub_col > j, col * inv_root, 0.0)
        lrow = jnp.where(lane_row >= j, row * inv_root, 0.0)
        s_ref[...] = a - lcol * lrow
        wrow = w_ref[pl.ds(j, 1), :] * inv_root
        w_ref[...] = w_ref[...] - lcol * wrow
        w_ref[pl.ds(j, 1), :] = wrow
        return carry

    lax.fori_loop(0, n, step, 0)


def _chol_inverse(block):
    n = block.shape[0]
    return pl.pallas_call(
        _leaf_kernel,
        out_shape=jax.ShapeDtypeStruct((n, n), jnp.float32),
        in_specs=[pl.BlockSpec(memory_space=pltpu.VMEM)],
        out_specs=pl.BlockSpec(memory_space=pltpu.VMEM),
        scratch_shapes=[pltpu.VMEM((n, n), jnp.float32)],
        cost_estimate=pl.CostEstimate(flops=6 * n * n * n, bytes_accessed=8 * n * n,
                                      transcendentals=n),
    )(block)


def precondition_blocks(blocks, nb, total_rows):
    block = blocks.shape[-1]
    na = nb - 1
    index = {p: k for k, p in enumerate(_tri_pairs(nb))}
    zero = len(index)
    pick = np.array([[index[(i, j)] if i >= j else zero for j in range(na)] for i in range(nb)],
                    dtype=np.int32)
    scale = 1.0 / total_rows
    tiles = blocks[pick] * scale
    work = tiles.transpose(0, 2, 1, 3).reshape(nb * block, na * block)
    eye = jnp.eye(block, dtype=blocks.dtype)
    grad_factor = blocks[index[(na, na)]] * scale + damping * eye
    inverses = []
    for k in range(na):
        lo = k * block
        hi = lo + block
        diag = work[lo:hi, lo:hi] + damping * eye
        inverse = _chol_inverse(diag)
        inverses.append(inverse)
        panel = _mm_nt(work[hi:, lo:hi], inverse)
        work = work.at[hi:, lo:hi].set(panel)
        if k + 1 < na:
            update = _mm_nt(panel, panel[: (na - k - 1) * block])
            work = work.at[hi:, hi:].add(-update)
    solved_t = work[na * block:, :]
    pieces = [None] * na
    for k in reversed(range(na)):
        lo = k * block
        hi = lo + block
        rhs = solved_t[:, lo:hi].T
        if k + 1 < na:
            below = jnp.concatenate(pieces[k + 1:], axis=0)
            rhs = rhs - _mm_t(work[hi:na * block, lo:hi], below)
        pieces[k] = _mm_t(inverses[k], rhs)
    left_solved = jnp.concatenate(pieces, axis=0)
    grad_inverse = _chol_inverse(grad_factor)
    return _mm(_mm_nt(left_solved, grad_inverse), grad_inverse)


def body(line_columns, line_widths, layer_owner):
    layer_count, positions, packed_width = line_columns.shape
    channels = packed_width // 4
    full_width = 10 * channels
    n_replicas = 1
    for axis in DP_AXES:
        n_replicas = n_replicas * lax.axis_size(axis)
    n_owners = lax.axis_size("owner")
    per_owner = layer_count // n_owners
    total_rows = n_replicas * n_owners * positions
    ordered = jnp.take(line_columns, layer_owner, axis=0)
    width_copies = jnp.broadcast_to(line_widths[None, :, :], (n_owners, 1, line_widths.shape[1]))
    received, source_widths = (
        lax.all_to_all(ordered, "owner", split_axis=0, concat_axis=1, tiled=True),
        lax.all_to_all(width_copies, "owner", split_axis=0, concat_axis=1, tiled=True),
    )
    blocks = received.reshape(per_owner, n_owners, positions, packed_width)
    columns = patch_columns(blocks, source_widths.reshape(n_owners, line_widths.shape[1]))
    columns = columns.reshape(n_owners * positions, full_width)
    gram = jnp.dot(columns.T, columns, preferred_element_type=jnp.float32)
    block = 128
    nb = full_width // block
    packed = pack_lower(gram, block)
    n_blocks = packed.shape[0]
    padded = -(-n_blocks * block // (8 * n_replicas)) * 8 * n_replicas // block
    packed = jnp.concatenate(
        [packed, jnp.zeros((padded - n_blocks, block, block), packed.dtype)], axis=0
    )
    chunk = padded * block // n_replicas
    packed = packed.reshape(n_replicas, chunk, block)
    mine = packed.reshape(padded * block, block)
    for axis in SCATTER_ORDER:
        mine = lax.psum_scatter(mine, axis, scatter_dimension=0, tiled=True)
    gathered = mine
    for axis in SCATTER_ORDER[::-1]:
        gathered = lax.all_gather(gathered, axis, axis=0, tiled=True)
    gathered = gathered.reshape(padded, block, block)
    results = precondition_blocks(gathered, nb, total_rows)[None]
    return lax.all_gather(results, "owner", axis=0, tiled=True)


DP_AXES = ("dp_x", "dp_z", "dp_y")
SCATTER_ORDER = ("dp_y", "dp_x", "dp_z")


def solution(mesh):
    dp_shape = (4, 2, mesh.shape["dp"] // 8)
    devices = mesh.devices.reshape(dp_shape + (mesh.shape["owner"],))
    fine = jax.sharding.Mesh(devices, DP_AXES + ("owner",))
    rows = DP_AXES + ("owner",)
    in_specs = (P(None, rows, None), P(rows, None), P())
    out_specs = P()
    return jax.shard_map(body, mesh=fine, in_specs=in_specs, out_specs=out_specs, check_vma=False)
```

```python
import numpy as np
import jax
import jax.numpy as jnp
from jax import lax
from jax.experimental import pallas as pl
from jax.experimental.pallas import tpu as pltpu
from jax.sharding import PartitionSpec as P

damping = 0.1


def patch_columns(block, widths):
    positions = block.shape[-2]
    channels = block.shape[-1] // 4
    line_ends = jnp.cumsum(widths, axis=-1).astype(jnp.int32)
    line_starts = line_ends - widths
    place = jnp.arange(positions, dtype=jnp.int32)[:, None]
    opening = jnp.any(place == line_starts[..., None, :], axis=-1)[..., None]
    closing = jnp.any(place + 1 == line_ends[..., None, :], axis=-1)[..., None]
    inside = place < line_ends[..., None, -1:]
    features = block[..., : 3 * channels]
    gradients = block[..., 3 * channels :]
    padding = jnp.zeros_like(features[..., :1, :])
    before = jnp.concatenate([padding, features[..., :-1, :]], axis=-2)
    after = jnp.concatenate([features[..., 1:, :], padding], axis=-2)
    before = jnp.where(opening, jnp.zeros_like(before), before)
    after = jnp.where(closing, jnp.zeros_like(after), after)
    stacked = jnp.concatenate([before, features, after, gradients], axis=-1)
    return jnp.where(inside, stacked, jnp.zeros_like(stacked))


def precondition(factor, total_rows):
    full_width = factor.shape[0]
    patch_width = full_width // 10 * 9
    scaled = factor / total_rows
    act_factor = scaled[:patch_width, :patch_width] + damping * jnp.eye(
        patch_width, dtype=factor.dtype
    )
    grad_factor = scaled[patch_width:, patch_width:] + damping * jnp.eye(
        full_width - patch_width, dtype=factor.dtype
    )
    cross_term = scaled[:patch_width, patch_width:]
    act_cholesky = jnp.linalg.cholesky(act_factor)
    left_solved = jax.scipy.linalg.cho_solve((act_cholesky, True), cross_term)
    grad_cholesky = jnp.linalg.cholesky(grad_factor)
    return jax.scipy.linalg.cho_solve((grad_cholesky, True), left_solved.T).T


def _tri_pairs(nb):
    return [(i, j) for j in range(nb) for i in range(j, nb)]


def pack_lower(gram, block):
    nb = gram.shape[0] // block
    tiles = gram.reshape(nb, block, nb, block).transpose(0, 2, 1, 3)
    pairs = _tri_pairs(nb)
    rows = np.array([p[0] for p in pairs], dtype=np.int32)
    cols = np.array([p[1] for p in pairs], dtype=np.int32)
    return tiles[rows, cols]


def unpack_lower(blocks, nb):
    block = blocks.shape[-1]
    index = {p: k for k, p in enumerate(_tri_pairs(nb))}
    pick = np.array([[index[(max(i, j), min(i, j))] for j in range(nb)] for i in range(nb)], dtype=np.int32)
    upper = np.array([[i < j for j in range(nb)] for i in range(nb)])
    tiles = blocks[pick]
    tiles = jnp.where(upper[:, :, None, None], jnp.swapaxes(tiles, -1, -2), tiles)
    return tiles.transpose(0, 2, 1, 3).reshape(nb * block, nb * block)


HIGH = lax.Precision.HIGHEST


def _mm(a, b):
    return jnp.dot(a, b, precision=HIGH, preferred_element_type=jnp.float32)


def _mm_t(a, b):
    return lax.dot_general(a, b, (((0,), (0,)), ((), ())), precision=HIGH,
                           preferred_element_type=jnp.float32)


def _mm_nt(a, b):
    return lax.dot_general(a, b, (((1,), (1,)), ((), ())), precision=HIGH,
                           preferred_element_type=jnp.float32)


def _chol_inv(block):
    lower = jnp.linalg.cholesky(block, symmetrize_input=False)
    eye = jnp.eye(block.shape[0], dtype=block.dtype)
    inverse = lax.linalg.triangular_solve(lower, eye, left_side=True, lower=True)
    return lower, inverse


def _leaf_kernel(a_ref, w_ref, s_ref):
    n = a_ref.shape[0]
    s_ref[...] = a_ref[...]
    sub = lax.broadcasted_iota(jnp.int32, (n, n), 0)
    lane = lax.broadcasted_iota(jnp.int32, (n, n), 1)
    w_ref[...] = jnp.where(sub == lane, 1.0, 0.0).astype(jnp.float32)
    lane_row = lax.broadcasted_iota(jnp.int32, (1, n), 1)
    sub_col = lax.broadcasted_iota(jnp.int32, (n, 1), 0)

    def step(j, carry):
        a = s_ref[...]
        row = s_ref[pl.ds(j, 1), :]
        pivot = jnp.sum(jnp.where(lane_row == j, row, 0.0), axis=1, keepdims=True)
        inv_root = 1.0 / jnp.sqrt(pivot)
        col = jnp.sum(jnp.where(lane == j, a, 0.0), axis=1, keepdims=True)
        lcol = jnp.where(sub_col > j, col * inv_root, 0.0)
        lrow = jnp.where(lane_row >= j, row * inv_root, 0.0)
        s_ref[...] = a - lcol * lrow
        wrow = w_ref[pl.ds(j, 1), :] * inv_root
        w_ref[...] = w_ref[...] - lcol * wrow
        w_ref[pl.ds(j, 1), :] = wrow
        return carry

    lax.fori_loop(0, n, step, 0)


def _chol_inverse(block):
    n = block.shape[0]
    return pl.pallas_call(
        _leaf_kernel,
        out_shape=jax.ShapeDtypeStruct((n, n), jnp.float32),
        in_specs=[pl.BlockSpec(memory_space=pltpu.VMEM)],
        out_specs=pl.BlockSpec(memory_space=pltpu.VMEM),
        scratch_shapes=[pltpu.VMEM((n, n), jnp.float32)],
        cost_estimate=pl.CostEstimate(flops=6 * n * n * n, bytes_accessed=8 * n * n,
                                      transcendentals=n),
    )(block)


def precondition_blocks(blocks, nb, total_rows):
    block = blocks.shape[-1]
    na = nb - 1
    index = {p: k for k, p in enumerate(_tri_pairs(nb))}
    scale = 1.0 / total_rows
    flat = blocks.reshape(-1, block)
    panels = []
    for j in range(na):
        start = index[(j, j)] * block
        panel = flat[start:start + (nb - j) * block]
        panels.append(jnp.pad(panel, ((j * block, 0), (0, 0))))
    work = jnp.concatenate(panels, axis=1) * scale
    eye = jnp.eye(block, dtype=blocks.dtype)
    grad_factor = blocks[index[(na, na)]] * scale + damping * eye
    inverses = []
    for k in range(na):
        lo = k * block
        hi = lo + block
        diag = work[lo:hi, lo:hi] + damping * eye
        inverse = _chol_inverse(diag)
        inverses.append(inverse)
        panel = _mm_nt(work[hi:, lo:hi], inverse)
        work = work.at[hi:, lo:hi].set(panel)
        if k + 1 < na:
            update = _mm_nt(panel, panel[: (na - k - 1) * block])
            work = work.at[hi:, hi:].add(-update)
    solved_t = work[na * block:, :]
    pieces = [None] * na
    for k in reversed(range(na)):
        lo = k * block
        hi = lo + block
        rhs = solved_t[:, lo:hi].T
        if k + 1 < na:
            below = jnp.concatenate(pieces[k + 1:], axis=0)
            rhs = rhs - _mm_t(work[hi:na * block, lo:hi], below)
        pieces[k] = _mm_t(inverses[k], rhs)
    left_solved = jnp.concatenate(pieces, axis=0)
    grad_inverse = _chol_inverse(grad_factor)
    return _mm(_mm_nt(left_solved, grad_inverse), grad_inverse)


def body(line_columns, line_widths, layer_owner):
    layer_count, positions, packed_width = line_columns.shape
    channels = packed_width // 4
    full_width = 10 * channels
    n_replicas = 1
    for axis in DP_AXES:
        n_replicas = n_replicas * lax.axis_size(axis)
    n_owners = lax.axis_size("owner")
    per_owner = layer_count // n_owners
    total_rows = n_replicas * n_owners * positions
    ordered = jnp.take(line_columns, layer_owner, axis=0)
    width_copies = jnp.broadcast_to(line_widths[None, :, :], (n_owners, 1, line_widths.shape[1]))
    received, source_widths = (
        lax.all_to_all(ordered, "owner", split_axis=0, concat_axis=1, tiled=True),
        lax.all_to_all(width_copies, "owner", split_axis=0, concat_axis=1, tiled=True),
    )
    blocks = received.reshape(per_owner, n_owners, positions, packed_width)
    columns = patch_columns(blocks, source_widths.reshape(n_owners, line_widths.shape[1]))
    columns = columns.reshape(n_owners * positions, full_width)
    gram = jnp.dot(columns.T, columns, preferred_element_type=jnp.float32)
    block = 128
    nb = full_width // block
    packed = pack_lower(gram, block)
    n_blocks = packed.shape[0]
    padded = -(-n_blocks * block // (8 * n_replicas)) * 8 * n_replicas // block
    packed = jnp.concatenate(
        [packed, jnp.zeros((padded - n_blocks, block, block), packed.dtype)], axis=0
    )
    chunk = padded * block // n_replicas
    packed = packed.reshape(n_replicas, chunk, block)
    mine = packed.reshape(padded * block, block)
    for axis in SCATTER_ORDER:
        mine = lax.psum_scatter(mine, axis, scatter_dimension=0, tiled=True)
    gathered = mine
    for axis in SCATTER_ORDER[::-1]:
        gathered = lax.all_gather(gathered, axis, axis=0, tiled=True)
    gathered = gathered.reshape(padded, block, block)
    results = precondition_blocks(gathered, nb, total_rows)[None]
    return lax.all_gather(results, "owner", axis=0, tiled=True)


DP_AXES = ("dp_x", "dp_z", "dp_y")
SCATTER_ORDER = ("dp_y", "dp_x", "dp_z")


def solution(mesh):
    dp_shape = (4, 2, mesh.shape["dp"] // 8)
    devices = mesh.devices.reshape(dp_shape + (mesh.shape["owner"],))
    fine = jax.sharding.Mesh(devices, DP_AXES + ("owner",))
    rows = DP_AXES + ("owner",)
    in_specs = (P(None, rows, None), P(rows, None), P())
    out_specs = P()
    return jax.shard_map(body, mesh=fine, in_specs=in_specs, out_specs=out_specs, check_vma=False)
```

```python
import numpy as np
import jax
import jax.numpy as jnp
from jax import lax
from jax.experimental import pallas as pl
from jax.experimental.pallas import tpu as pltpu
from jax.sharding import PartitionSpec as P

damping = 0.1


def patch_columns(block, widths):
    positions = block.shape[-2]
    channels = block.shape[-1] // 4
    line_ends = jnp.cumsum(widths, axis=-1).astype(jnp.int32)
    line_starts = line_ends - widths
    place = jnp.arange(positions, dtype=jnp.int32)[:, None]
    opening = jnp.any(place == line_starts[..., None, :], axis=-1)[..., None]
    closing = jnp.any(place + 1 == line_ends[..., None, :], axis=-1)[..., None]
    inside = place < line_ends[..., None, -1:]
    features = block[..., : 3 * channels]
    gradients = block[..., 3 * channels :]
    padding = jnp.zeros_like(features[..., :1, :])
    before = jnp.concatenate([padding, features[..., :-1, :]], axis=-2)
    after = jnp.concatenate([features[..., 1:, :], padding], axis=-2)
    before = jnp.where(opening, jnp.zeros_like(before), before)
    after = jnp.where(closing, jnp.zeros_like(after), after)
    stacked = jnp.concatenate([before, features, after, gradients], axis=-1)
    return jnp.where(inside, stacked, jnp.zeros_like(stacked))


def precondition(factor, total_rows):
    full_width = factor.shape[0]
    patch_width = full_width // 10 * 9
    scaled = factor / total_rows
    act_factor = scaled[:patch_width, :patch_width] + damping * jnp.eye(
        patch_width, dtype=factor.dtype
    )
    grad_factor = scaled[patch_width:, patch_width:] + damping * jnp.eye(
        full_width - patch_width, dtype=factor.dtype
    )
    cross_term = scaled[:patch_width, patch_width:]
    act_cholesky = jnp.linalg.cholesky(act_factor)
    left_solved = jax.scipy.linalg.cho_solve((act_cholesky, True), cross_term)
    grad_cholesky = jnp.linalg.cholesky(grad_factor)
    return jax.scipy.linalg.cho_solve((grad_cholesky, True), left_solved.T).T


def _tri_pairs(nb):
    return [(i, j) for j in range(nb) for i in range(j, nb)]


def pack_lower(gram, block):
    nb = gram.shape[0] // block
    tiles = gram.reshape(nb, block, nb, block).transpose(0, 2, 1, 3)
    pairs = _tri_pairs(nb)
    rows = np.array([p[0] for p in pairs], dtype=np.int32)
    cols = np.array([p[1] for p in pairs], dtype=np.int32)
    return tiles[rows, cols]


def unpack_lower(blocks, nb):
    block = blocks.shape[-1]
    index = {p: k for k, p in enumerate(_tri_pairs(nb))}
    pick = np.array([[index[(max(i, j), min(i, j))] for j in range(nb)] for i in range(nb)], dtype=np.int32)
    upper = np.array([[i < j for j in range(nb)] for i in range(nb)])
    tiles = blocks[pick]
    tiles = jnp.where(upper[:, :, None, None], jnp.swapaxes(tiles, -1, -2), tiles)
    return tiles.transpose(0, 2, 1, 3).reshape(nb * block, nb * block)


HIGH = lax.Precision.HIGHEST


def _mm(a, b):
    return jnp.dot(a, b, precision=HIGH, preferred_element_type=jnp.float32)


def _mm_t(a, b):
    return lax.dot_general(a, b, (((0,), (0,)), ((), ())), precision=HIGH,
                           preferred_element_type=jnp.float32)


def _mm_nt(a, b):
    return lax.dot_general(a, b, (((1,), (1,)), ((), ())), precision=HIGH,
                           preferred_element_type=jnp.float32)


def _chol_inv(block):
    lower = jnp.linalg.cholesky(block, symmetrize_input=False)
    eye = jnp.eye(block.shape[0], dtype=block.dtype)
    inverse = lax.linalg.triangular_solve(lower, eye, left_side=True, lower=True)
    return lower, inverse


def _leaf_kernel(a_ref, w_ref, s_ref):
    n = a_ref.shape[0]
    s_ref[...] = a_ref[...]
    sub = lax.broadcasted_iota(jnp.int32, (n, n), 0)
    lane = lax.broadcasted_iota(jnp.int32, (n, n), 1)
    w_ref[...] = jnp.where(sub == lane, 1.0, 0.0).astype(jnp.float32)
    lane_row = lax.broadcasted_iota(jnp.int32, (1, n), 1)
    sub_col = lax.broadcasted_iota(jnp.int32, (n, 1), 0)

    def step(j, carry):
        a = s_ref[...]
        row = s_ref[pl.ds(j, 1), :]
        pivot = jnp.sum(jnp.where(lane_row == j, row, 0.0), axis=1, keepdims=True)
        inv_root = 1.0 / jnp.sqrt(pivot)
        col = jnp.sum(jnp.where(lane == j, a, 0.0), axis=1, keepdims=True)
        lcol = jnp.where(sub_col > j, col * inv_root, 0.0)
        lrow = jnp.where(lane_row >= j, row * inv_root, 0.0)
        s_ref[...] = a - lcol * lrow
        wrow = w_ref[pl.ds(j, 1), :] * inv_root
        w_ref[...] = w_ref[...] - lcol * wrow
        w_ref[pl.ds(j, 1), :] = wrow
        return carry

    lax.fori_loop(0, n, step, 0)


def _chol_inverse(block):
    n = block.shape[0]
    return pl.pallas_call(
        _leaf_kernel,
        out_shape=jax.ShapeDtypeStruct((n, n), jnp.float32),
        in_specs=[pl.BlockSpec(memory_space=pltpu.VMEM)],
        out_specs=pl.BlockSpec(memory_space=pltpu.VMEM),
        scratch_shapes=[pltpu.VMEM((n, n), jnp.float32)],
        cost_estimate=pl.CostEstimate(flops=6 * n * n * n, bytes_accessed=8 * n * n,
                                      transcendentals=n),
    )(block)


def precondition_blocks(blocks, nb, total_rows):
    block = blocks.shape[-1]
    na = nb - 1
    index = {p: k for k, p in enumerate(_tri_pairs(nb))}
    scale = 1.0 / total_rows
    flat = blocks.reshape(-1, block)
    panels = []
    for j in range(na):
        start = index[(j, j)] * block
        panel = flat[start:start + (nb - j) * block]
        panels.append(jnp.pad(panel, ((j * block, 0), (0, 0))))
    work = jnp.concatenate(panels, axis=1) * scale
    eye = jnp.eye(block, dtype=blocks.dtype)
    grad_factor = blocks[index[(na, na)]] * scale + damping * eye
    inverses = []
    for k in range(na):
        lo = k * block
        hi = lo + block
        diag = work[lo:hi, lo:hi] + damping * eye
        inverse = _chol_inverse(diag)
        inverses.append(inverse)
        panel = _mm_nt(work[hi:, lo:hi], inverse)
        work = work.at[hi:, lo:hi].set(panel)
        if k + 1 < na:
            update = _mm_nt(panel, panel[: (na - k - 1) * block])
            work = work.at[hi:, hi:].add(-update)
    solved_t = work[na * block:, :]
    pieces = [None] * na
    for k in reversed(range(na)):
        lo = k * block
        hi = lo + block
        rhs = solved_t[:, lo:hi].T
        if k + 1 < na:
            below = jnp.concatenate(pieces[k + 1:], axis=0)
            rhs = rhs - _mm_t(work[hi:na * block, lo:hi], below)
        pieces[k] = _mm_t(inverses[k], rhs)
    left_solved = jnp.concatenate(pieces, axis=0)
    grad_inverse = _chol_inverse(grad_factor)
    return _mm(_mm_nt(left_solved, grad_inverse), grad_inverse)


def body(line_columns, line_widths, layer_owner):
    layer_count, positions, packed_width = line_columns.shape
    channels = packed_width // 4
    full_width = 10 * channels
    n_replicas = 1
    for axis in DP_AXES:
        n_replicas = n_replicas * lax.axis_size(axis)
    n_owners = lax.axis_size(OWNER_AXES[0]) * lax.axis_size(OWNER_AXES[1])
    per_owner = layer_count // n_owners
    total_rows = n_replicas * n_owners * positions
    ordered = jnp.take(line_columns, layer_owner, axis=0)
    width_copies = jnp.broadcast_to(line_widths[None, :, :], (n_owners, 1, line_widths.shape[1]))
    received, source_widths = (
        lax.all_to_all(ordered, OWNER_AXES, split_axis=0, concat_axis=1, tiled=True),
        lax.all_to_all(width_copies, OWNER_AXES, split_axis=0, concat_axis=1, tiled=True),
    )
    blocks = received.reshape(per_owner, n_owners, positions, packed_width)
    columns = patch_columns(blocks, source_widths.reshape(n_owners, line_widths.shape[1]))
    columns = columns.reshape(n_owners * positions, full_width)
    block = 128
    nb = full_width // block
    n_blocks = nb * (nb + 1) // 2
    padded = -(-n_blocks * block // (8 * n_replicas)) * 8 * n_replicas // block
    panels = [
        lax.dot_general(columns[:, j * block:], columns[:, j * block:(j + 1) * block],
                        (((0,), (0,)), ((), ())), preferred_element_type=jnp.float32)
        for j in range(nb)
    ]
    panels.append(jnp.zeros(((padded - n_blocks) * block, block), jnp.float32))
    mine = jnp.concatenate(panels, axis=0)
    for axis in SCATTER_ORDER:
        mine = lax.psum_scatter(mine, axis, scatter_dimension=0, tiled=True)
    gathered = mine
    for axis in SCATTER_ORDER[::-1]:
        gathered = lax.all_gather(gathered, axis, axis=0, tiled=True)
    gathered = gathered.reshape(padded, block, block)
    results = precondition_blocks(gathered, nb, total_rows)[None]
    results = lax.all_gather(results, OWNER_AXES[0], axis=0, tiled=True)
    results = lax.all_gather(results, OWNER_AXES[1], axis=1, tiled=False)
    return results.reshape((n_owners,) + results.shape[2:])


DP_AXES = ("dp_x", "dp_z", "dp_y")
SCATTER_ORDER = ("dp_y", "dp_x", "dp_z")


OWNER_AXES = ("owner_z", "owner_c")


def solution(mesh):
    dp_shape = (4, 2, mesh.shape["dp"] // 8)
    owner_shape = (mesh.shape["owner"] // 2, 2)
    devices = mesh.devices.reshape(dp_shape + owner_shape)
    fine = jax.sharding.Mesh(devices, DP_AXES + OWNER_AXES)
    rows = DP_AXES + OWNER_AXES
    in_specs = (P(None, rows, None), P(rows, None), P())
    out_specs = P()
    return jax.shard_map(body, mesh=fine, in_specs=in_specs, out_specs=out_specs, check_vma=False)
```

```python
import numpy as np
import jax
import jax.numpy as jnp
from jax import lax
from jax.experimental import pallas as pl
from jax.experimental.pallas import tpu as pltpu
from jax.sharding import PartitionSpec as P

damping = 0.1


def patch_columns(block, widths):
    positions = block.shape[-2]
    channels = block.shape[-1] // 4
    line_ends = jnp.cumsum(widths, axis=-1).astype(jnp.int32)
    line_starts = line_ends - widths
    place = jnp.arange(positions, dtype=jnp.int32)[:, None]
    opening = jnp.any(place == line_starts[..., None, :], axis=-1)[..., None]
    closing = jnp.any(place + 1 == line_ends[..., None, :], axis=-1)[..., None]
    inside = place < line_ends[..., None, -1:]
    features = block[..., : 3 * channels]
    gradients = block[..., 3 * channels :]
    padding = jnp.zeros_like(features[..., :1, :])
    before = jnp.concatenate([padding, features[..., :-1, :]], axis=-2)
    after = jnp.concatenate([features[..., 1:, :], padding], axis=-2)
    before = jnp.where(opening, jnp.zeros_like(before), before)
    after = jnp.where(closing, jnp.zeros_like(after), after)
    stacked = jnp.concatenate([before, features, after, gradients], axis=-1)
    return jnp.where(inside, stacked, jnp.zeros_like(stacked))


def precondition(factor, total_rows):
    full_width = factor.shape[0]
    patch_width = full_width // 10 * 9
    scaled = factor / total_rows
    act_factor = scaled[:patch_width, :patch_width] + damping * jnp.eye(
        patch_width, dtype=factor.dtype
    )
    grad_factor = scaled[patch_width:, patch_width:] + damping * jnp.eye(
        full_width - patch_width, dtype=factor.dtype
    )
    cross_term = scaled[:patch_width, patch_width:]
    act_cholesky = jnp.linalg.cholesky(act_factor)
    left_solved = jax.scipy.linalg.cho_solve((act_cholesky, True), cross_term)
    grad_cholesky = jnp.linalg.cholesky(grad_factor)
    return jax.scipy.linalg.cho_solve((grad_cholesky, True), left_solved.T).T


def _tri_pairs(nb):
    return [(i, j) for j in range(nb) for i in range(j, nb)]


def pack_lower(gram, block):
    nb = gram.shape[0] // block
    tiles = gram.reshape(nb, block, nb, block).transpose(0, 2, 1, 3)
    pairs = _tri_pairs(nb)
    rows = np.array([p[0] for p in pairs], dtype=np.int32)
    cols = np.array([p[1] for p in pairs], dtype=np.int32)
    return tiles[rows, cols]


def unpack_lower(blocks, nb):
    block = blocks.shape[-1]
    index = {p: k for k, p in enumerate(_tri_pairs(nb))}
    pick = np.array([[index[(max(i, j), min(i, j))] for j in range(nb)] for i in range(nb)], dtype=np.int32)
    upper = np.array([[i < j for j in range(nb)] for i in range(nb)])
    tiles = blocks[pick]
    tiles = jnp.where(upper[:, :, None, None], jnp.swapaxes(tiles, -1, -2), tiles)
    return tiles.transpose(0, 2, 1, 3).reshape(nb * block, nb * block)


HIGH = lax.Precision.HIGHEST


def _mm(a, b):
    return jnp.dot(a, b, precision=HIGH, preferred_element_type=jnp.float32)


def _mm_t(a, b):
    return lax.dot_general(a, b, (((0,), (0,)), ((), ())), precision=HIGH,
                           preferred_element_type=jnp.float32)


def _mm_nt(a, b):
    return lax.dot_general(a, b, (((1,), (1,)), ((), ())), precision=HIGH,
                           preferred_element_type=jnp.float32)


def _chol_inv(block):
    lower = jnp.linalg.cholesky(block, symmetrize_input=False)
    eye = jnp.eye(block.shape[0], dtype=block.dtype)
    inverse = lax.linalg.triangular_solve(lower, eye, left_side=True, lower=True)
    return lower, inverse


def _leaf_kernel(a_ref, w_ref, s_ref):
    n = a_ref.shape[0]
    s_ref[...] = a_ref[...]
    sub = lax.broadcasted_iota(jnp.int32, (n, n), 0)
    lane = lax.broadcasted_iota(jnp.int32, (n, n), 1)
    w_ref[...] = jnp.where(sub == lane, 1.0, 0.0).astype(jnp.float32)
    lane_row = lax.broadcasted_iota(jnp.int32, (1, n), 1)
    sub_col = lax.broadcasted_iota(jnp.int32, (n, 1), 0)

    def step(j, carry):
        a = s_ref[...]
        row = s_ref[pl.ds(j, 1), :]
        pivot = jnp.sum(jnp.where(lane_row == j, row, 0.0), axis=1, keepdims=True)
        inv_root = 1.0 / jnp.sqrt(pivot)
        col = jnp.sum(jnp.where(lane == j, a, 0.0), axis=1, keepdims=True)
        lcol = jnp.where(sub_col > j, col * inv_root, 0.0)
        lrow = jnp.where(lane_row >= j, row * inv_root, 0.0)
        s_ref[...] = a - lcol * lrow
        wrow = w_ref[pl.ds(j, 1), :] * inv_root
        w_ref[...] = w_ref[...] - lcol * wrow
        w_ref[pl.ds(j, 1), :] = wrow
        return carry

    lax.fori_loop(0, n, step, 0)


def _chol_inverse(block):
    n = block.shape[0]
    return pl.pallas_call(
        _leaf_kernel,
        out_shape=jax.ShapeDtypeStruct((n, n), jnp.float32),
        in_specs=[pl.BlockSpec(memory_space=pltpu.VMEM)],
        out_specs=pl.BlockSpec(memory_space=pltpu.VMEM),
        scratch_shapes=[pltpu.VMEM((n, n), jnp.float32)],
        cost_estimate=pl.CostEstimate(flops=6 * n * n * n, bytes_accessed=8 * n * n,
                                      transcendentals=n),
    )(block)


def precondition_blocks(blocks, nb, total_rows):
    block = blocks.shape[-1]
    na = nb - 1
    index = {p: k for k, p in enumerate(_tri_pairs(nb))}
    scale = 1.0 / total_rows
    flat = blocks.reshape(-1, block)
    panels = []
    for j in range(na):
        start = index[(j, j)] * block
        panel = flat[start:start + (nb - j) * block]
        panels.append(jnp.pad(panel, ((j * block, 0), (0, 0))))
    work = jnp.concatenate(panels, axis=1) * scale
    eye = jnp.eye(block, dtype=blocks.dtype)
    grad_factor = blocks[index[(na, na)]] * scale + damping * eye
    inverses = []
    for k in range(na):
        lo = k * block
        hi = lo + block
        diag = work[lo:hi, lo:hi] + damping * eye
        inverse = _chol_inverse(diag)
        inverses.append(inverse)
        panel = _mm_nt(work[hi:, lo:hi], inverse)
        work = work.at[hi:, lo:hi].set(panel)
        if k + 1 < na:
            update = _mm_nt(panel, panel[: (na - k - 1) * block])
            work = work.at[hi:, hi:].add(-update)
    solved_t = work[na * block:, :]
    pieces = [None] * na
    for k in reversed(range(na)):
        lo = k * block
        hi = lo + block
        rhs = solved_t[:, lo:hi].T
        if k + 1 < na:
            below = jnp.concatenate(pieces[k + 1:], axis=0)
            rhs = rhs - _mm_t(work[hi:na * block, lo:hi], below)
        pieces[k] = _mm_t(inverses[k], rhs)
    left_solved = jnp.concatenate(pieces, axis=0)
    grad_inverse = _chol_inverse(grad_factor)
    return _mm(_mm_nt(left_solved, grad_inverse), grad_inverse)


def body(line_columns, line_widths, layer_owner):
    layer_count, positions, packed_width = line_columns.shape
    channels = packed_width // 4
    full_width = 10 * channels
    n_replicas = 1
    for axis in DP_AXES:
        n_replicas = n_replicas * lax.axis_size(axis)
    n_owners = lax.axis_size(OWNER_AXES[0]) * lax.axis_size(OWNER_AXES[1])
    per_owner = layer_count // n_owners
    total_rows = n_replicas * n_owners * positions
    ordered = jnp.take(line_columns, layer_owner, axis=0)
    width_copies = jnp.broadcast_to(line_widths[None, :, :], (n_owners, 1, line_widths.shape[1]))
    received, source_widths = (
        lax.all_to_all(ordered, OWNER_AXES, split_axis=0, concat_axis=1, tiled=True),
        lax.all_to_all(width_copies, OWNER_AXES, split_axis=0, concat_axis=1, tiled=True),
    )
    blocks = received.reshape(per_owner, n_owners, positions, packed_width)
    columns = patch_columns(blocks, source_widths.reshape(n_owners, line_widths.shape[1]))
    columns = columns.reshape(n_owners * positions, full_width)
    block = 128
    nb = full_width // block
    n_blocks = nb * (nb + 1) // 2
    padded = -(-n_blocks * block // (8 * n_replicas)) * 8 * n_replicas // block
    panels = [
        lax.dot_general(columns[:, j * block:], columns[:, j * block:(j + 1) * block],
                        (((0,), (0,)), ((), ())), preferred_element_type=jnp.float32)
        for j in range(nb)
    ]
    panels.append(jnp.zeros(((padded - n_blocks) * block, block), jnp.float32))
    mine = jnp.concatenate(panels, axis=0)
    for axis in SCATTER_ORDER:
        mine = lax.psum_scatter(mine, axis, scatter_dimension=0, tiled=True)
    gathered = mine
    for axis in SCATTER_ORDER[::-1]:
        gathered = lax.all_gather(gathered, axis, axis=0, tiled=True)
    gathered = gathered.reshape(padded, block, block)
    results = precondition_blocks(gathered, nb, total_rows)[None]
    return lax.all_gather(results, OWNER_AXES, axis=0, tiled=True)


DP_AXES = ("dp_x", "dp_z", "dp_y")
SCATTER_ORDER = ("dp_y", "dp_x", "dp_z")


OWNER_AXES = ("owner_z", "owner_c")


def solution(mesh):
    dp_shape = (4, 2, mesh.shape["dp"] // 8)
    owner_shape = (mesh.shape["owner"] // 2, 2)
    devices = mesh.devices.reshape(dp_shape + owner_shape)
    fine = jax.sharding.Mesh(devices, DP_AXES + OWNER_AXES)
    rows = DP_AXES + OWNER_AXES
    in_specs = (P(None, rows, None), P(rows, None), P())
    out_specs = P()
    return jax.shard_map(body, mesh=fine, in_specs=in_specs, out_specs=out_specs, check_vma=False)
```

```python
import numpy as np
import jax
import jax.numpy as jnp
from jax import lax
from jax.experimental import pallas as pl
from jax.experimental.pallas import tpu as pltpu
from jax.sharding import PartitionSpec as P

damping = 0.1


def patch_columns(block, widths):
    positions = block.shape[-2]
    channels = block.shape[-1] // 4
    line_ends = jnp.cumsum(widths, axis=-1).astype(jnp.int32)
    line_starts = line_ends - widths
    place = jnp.arange(positions, dtype=jnp.int32)[:, None]
    opening = jnp.any(place == line_starts[..., None, :], axis=-1)[..., None]
    closing = jnp.any(place + 1 == line_ends[..., None, :], axis=-1)[..., None]
    inside = place < line_ends[..., None, -1:]
    features = block[..., : 3 * channels]
    gradients = block[..., 3 * channels :]
    padding = jnp.zeros_like(features[..., :1, :])
    before = jnp.concatenate([padding, features[..., :-1, :]], axis=-2)
    after = jnp.concatenate([features[..., 1:, :], padding], axis=-2)
    before = jnp.where(opening, jnp.zeros_like(before), before)
    after = jnp.where(closing, jnp.zeros_like(after), after)
    stacked = jnp.concatenate([before, features, after, gradients], axis=-1)
    return jnp.where(inside, stacked, jnp.zeros_like(stacked))


def precondition(factor, total_rows):
    full_width = factor.shape[0]
    patch_width = full_width // 10 * 9
    scaled = factor / total_rows
    act_factor = scaled[:patch_width, :patch_width] + damping * jnp.eye(
        patch_width, dtype=factor.dtype
    )
    grad_factor = scaled[patch_width:, patch_width:] + damping * jnp.eye(
        full_width - patch_width, dtype=factor.dtype
    )
    cross_term = scaled[:patch_width, patch_width:]
    act_cholesky = jnp.linalg.cholesky(act_factor)
    left_solved = jax.scipy.linalg.cho_solve((act_cholesky, True), cross_term)
    grad_cholesky = jnp.linalg.cholesky(grad_factor)
    return jax.scipy.linalg.cho_solve((grad_cholesky, True), left_solved.T).T


def _tri_pairs(nb):
    return [(i, j) for j in range(nb) for i in range(j, nb)]


def pack_lower(gram, block):
    nb = gram.shape[0] // block
    tiles = gram.reshape(nb, block, nb, block).transpose(0, 2, 1, 3)
    pairs = _tri_pairs(nb)
    rows = np.array([p[0] for p in pairs], dtype=np.int32)
    cols = np.array([p[1] for p in pairs], dtype=np.int32)
    return tiles[rows, cols]


def unpack_lower(blocks, nb):
    block = blocks.shape[-1]
    index = {p: k for k, p in enumerate(_tri_pairs(nb))}
    pick = np.array([[index[(max(i, j), min(i, j))] for j in range(nb)] for i in range(nb)], dtype=np.int32)
    upper = np.array([[i < j for j in range(nb)] for i in range(nb)])
    tiles = blocks[pick]
    tiles = jnp.where(upper[:, :, None, None], jnp.swapaxes(tiles, -1, -2), tiles)
    return tiles.transpose(0, 2, 1, 3).reshape(nb * block, nb * block)


HIGH = lax.Precision.HIGHEST


def _mm(a, b):
    return jnp.dot(a, b, precision=HIGH, preferred_element_type=jnp.float32)


def _mm_t(a, b):
    return lax.dot_general(a, b, (((0,), (0,)), ((), ())), precision=HIGH,
                           preferred_element_type=jnp.float32)


def _mm_nt(a, b):
    return lax.dot_general(a, b, (((1,), (1,)), ((), ())), precision=HIGH,
                           preferred_element_type=jnp.float32)


def _chol_inv(block):
    lower = jnp.linalg.cholesky(block, symmetrize_input=False)
    eye = jnp.eye(block.shape[0], dtype=block.dtype)
    inverse = lax.linalg.triangular_solve(lower, eye, left_side=True, lower=True)
    return lower, inverse


def _leaf_kernel(a_ref, w_ref, s_ref):
    n = a_ref.shape[0]
    s_ref[...] = a_ref[...]
    sub = lax.broadcasted_iota(jnp.int32, (n, n), 0)
    lane = lax.broadcasted_iota(jnp.int32, (n, n), 1)
    w_ref[...] = jnp.where(sub == lane, 1.0, 0.0).astype(jnp.float32)
    lane_row = lax.broadcasted_iota(jnp.int32, (1, n), 1)
    seg = 16
    for start in range(0, n, seg):
        rows = n - start
        lane_t = lax.broadcasted_iota(jnp.int32, (rows, n), 1)
        sub_col = lax.broadcasted_iota(jnp.int32, (rows, 1), 0) + start

        def step(j, carry, start=start, lane_t=lane_t, sub_col=sub_col):
            a = s_ref[start:, :]
            row = s_ref[pl.ds(j, 1), :]
            pivot = jnp.sum(jnp.where(lane_row == j, row, 0.0), axis=1, keepdims=True)
            inv_root = 1.0 / jnp.sqrt(pivot)
            col = jnp.sum(jnp.where(lane_t == j, a, 0.0), axis=1, keepdims=True)
            lcol = jnp.where(sub_col > j, col * inv_root, 0.0)
            lrow = jnp.where(lane_row >= j, row * inv_root, 0.0)
            s_ref[start:, :] = a - lcol * lrow
            wrow = w_ref[pl.ds(j, 1), :] * inv_root
            w_ref[start:, :] = w_ref[start:, :] - lcol * wrow
            w_ref[pl.ds(j, 1), :] = wrow
            return carry

        lax.fori_loop(start, start + seg, step, 0)

def _chol_inverse(block):
    n = block.shape[0]
    return pl.pallas_call(
        _leaf_kernel,
        out_shape=jax.ShapeDtypeStruct((n, n), jnp.float32),
        in_specs=[pl.BlockSpec(memory_space=pltpu.VMEM)],
        out_specs=pl.BlockSpec(memory_space=pltpu.VMEM),
        scratch_shapes=[pltpu.VMEM((n, n), jnp.float32)],
        cost_estimate=pl.CostEstimate(flops=6 * n * n * n, bytes_accessed=8 * n * n,
                                      transcendentals=n),
    )(block)


def precondition_blocks(blocks, nb, total_rows):
    block = blocks.shape[-1]
    na = nb - 1
    index = {p: k for k, p in enumerate(_tri_pairs(nb))}
    scale = 1.0 / total_rows
    flat = blocks.reshape(-1, block)
    panels = []
    for j in range(na):
        start = index[(j, j)] * block
        panel = flat[start:start + (nb - j) * block]
        panels.append(jnp.pad(panel, ((j * block, 0), (0, 0))))
    work = jnp.concatenate(panels, axis=1) * scale
    eye = jnp.eye(block, dtype=blocks.dtype)
    grad_factor = blocks[index[(na, na)]] * scale + damping * eye
    inverses = []
    for k in range(na):
        lo = k * block
        hi = lo + block
        diag = work[lo:hi, lo:hi] + damping * eye
        inverse = _chol_inverse(diag)
        inverses.append(inverse)
        panel = _mm_nt(work[hi:, lo:hi], inverse)
        work = work.at[hi:, lo:hi].set(panel)
        if k + 1 < na:
            update = _mm_nt(panel, panel[: (na - k - 1) * block])
            work = work.at[hi:, hi:].add(-update)
    solved_t = work[na * block:, :]
    pieces = [None] * na
    for k in reversed(range(na)):
        lo = k * block
        hi = lo + block
        rhs = solved_t[:, lo:hi].T
        if k + 1 < na:
            below = jnp.concatenate(pieces[k + 1:], axis=0)
            rhs = rhs - _mm_t(work[hi:na * block, lo:hi], below)
        pieces[k] = _mm_t(inverses[k], rhs)
    left_solved = jnp.concatenate(pieces, axis=0)
    grad_inverse = _chol_inverse(grad_factor)
    return _mm(_mm_nt(left_solved, grad_inverse), grad_inverse)


def body(line_columns, line_widths, layer_owner):
    layer_count, positions, packed_width = line_columns.shape
    channels = packed_width // 4
    full_width = 10 * channels
    n_replicas = 1
    for axis in DP_AXES:
        n_replicas = n_replicas * lax.axis_size(axis)
    n_owners = lax.axis_size(OWNER_AXES[0]) * lax.axis_size(OWNER_AXES[1])
    per_owner = layer_count // n_owners
    total_rows = n_replicas * n_owners * positions
    ordered = jnp.take(line_columns, layer_owner, axis=0, mode="clip")
    width_copies = jnp.broadcast_to(line_widths[None, :, :], (n_owners, 1, line_widths.shape[1]))
    received, source_widths = (
        lax.all_to_all(ordered, OWNER_AXES, split_axis=0, concat_axis=1, tiled=True),
        lax.all_to_all(width_copies, OWNER_AXES, split_axis=0, concat_axis=1, tiled=True),
    )
    blocks = received.reshape(per_owner, n_owners, positions, packed_width)
    columns = patch_columns(blocks, source_widths.reshape(n_owners, line_widths.shape[1]))
    columns = columns.reshape(n_owners * positions, full_width)
    block = 128
    nb = full_width // block
    n_blocks = nb * (nb + 1) // 2
    padded = -(-n_blocks * block // (8 * n_replicas)) * 8 * n_replicas // block
    panels = [
        lax.dot_general(columns[:, j * block:], columns[:, j * block:(j + 1) * block],
                        (((0,), (0,)), ((), ())), preferred_element_type=jnp.float32)
        for j in range(nb)
    ]
    panels.append(jnp.zeros(((padded - n_blocks) * block, block), jnp.float32))
    mine = jnp.concatenate(panels, axis=0)
    for axis in SCATTER_ORDER:
        mine = lax.psum_scatter(mine, axis, scatter_dimension=0, tiled=True)
    gathered = mine
    for axis in SCATTER_ORDER[::-1]:
        gathered = lax.all_gather(gathered, axis, axis=0, tiled=True)
    gathered = gathered.reshape(padded, block, block)
    results = precondition_blocks(gathered, nb, total_rows)[None]
    return lax.all_gather(results, OWNER_AXES, axis=0, tiled=True)


DP_AXES = ("dp_x", "dp_z", "dp_y")
SCATTER_ORDER = ("dp_y", "dp_x", "dp_z")


OWNER_AXES = ("owner_z", "owner_c")


def solution(mesh):
    dp_shape = (4, 2, mesh.shape["dp"] // 8)
    owner_shape = (mesh.shape["owner"] // 2, 2)
    devices = mesh.devices.reshape(dp_shape + owner_shape)
    fine = jax.sharding.Mesh(devices, DP_AXES + OWNER_AXES)
    rows = DP_AXES + OWNER_AXES
    in_specs = (P(None, rows, None), P(rows, None), P())
    out_specs = P()
    return jax.shard_map(body, mesh=fine, in_specs=in_specs, out_specs=out_specs, check_vma=False)
```

```python
import numpy as np
import jax
import jax.numpy as jnp
from jax import lax
from jax.experimental import pallas as pl
from jax.experimental.pallas import tpu as pltpu
from jax.sharding import PartitionSpec as P

damping = 0.1


def patch_columns(block, widths):
    positions = block.shape[-2]
    channels = block.shape[-1] // 4
    line_ends = jnp.cumsum(widths, axis=-1).astype(jnp.int32)
    line_starts = line_ends - widths
    place = jnp.arange(positions, dtype=jnp.int32)[:, None]
    opening = jnp.any(place == line_starts[..., None, :], axis=-1)[..., None]
    closing = jnp.any(place + 1 == line_ends[..., None, :], axis=-1)[..., None]
    inside = place < line_ends[..., None, -1:]
    features = block[..., : 3 * channels]
    gradients = block[..., 3 * channels :]
    padding = jnp.zeros_like(features[..., :1, :])
    before = jnp.concatenate([padding, features[..., :-1, :]], axis=-2)
    after = jnp.concatenate([features[..., 1:, :], padding], axis=-2)
    before = jnp.where(opening, jnp.zeros_like(before), before)
    after = jnp.where(closing, jnp.zeros_like(after), after)
    stacked = jnp.concatenate([before, features, after, gradients], axis=-1)
    return jnp.where(inside, stacked, jnp.zeros_like(stacked))


def precondition(factor, total_rows):
    full_width = factor.shape[0]
    patch_width = full_width // 10 * 9
    scaled = factor / total_rows
    act_factor = scaled[:patch_width, :patch_width] + damping * jnp.eye(
        patch_width, dtype=factor.dtype
    )
    grad_factor = scaled[patch_width:, patch_width:] + damping * jnp.eye(
        full_width - patch_width, dtype=factor.dtype
    )
    cross_term = scaled[:patch_width, patch_width:]
    act_cholesky = jnp.linalg.cholesky(act_factor)
    left_solved = jax.scipy.linalg.cho_solve((act_cholesky, True), cross_term)
    grad_cholesky = jnp.linalg.cholesky(grad_factor)
    return jax.scipy.linalg.cho_solve((grad_cholesky, True), left_solved.T).T


def _tri_pairs(nb):
    return [(i, j) for j in range(nb) for i in range(j, nb)]


def pack_lower(gram, block):
    nb = gram.shape[0] // block
    tiles = gram.reshape(nb, block, nb, block).transpose(0, 2, 1, 3)
    pairs = _tri_pairs(nb)
    rows = np.array([p[0] for p in pairs], dtype=np.int32)
    cols = np.array([p[1] for p in pairs], dtype=np.int32)
    return tiles[rows, cols]


def unpack_lower(blocks, nb):
    block = blocks.shape[-1]
    index = {p: k for k, p in enumerate(_tri_pairs(nb))}
    pick = np.array([[index[(max(i, j), min(i, j))] for j in range(nb)] for i in range(nb)], dtype=np.int32)
    upper = np.array([[i < j for j in range(nb)] for i in range(nb)])
    tiles = blocks[pick]
    tiles = jnp.where(upper[:, :, None, None], jnp.swapaxes(tiles, -1, -2), tiles)
    return tiles.transpose(0, 2, 1, 3).reshape(nb * block, nb * block)


HIGH = lax.Precision.HIGHEST


def _mm(a, b):
    return jnp.dot(a, b, precision=HIGH, preferred_element_type=jnp.float32)


def _mm_t(a, b):
    return lax.dot_general(a, b, (((0,), (0,)), ((), ())), precision=HIGH,
                           preferred_element_type=jnp.float32)


def _mm_nt(a, b):
    return lax.dot_general(a, b, (((1,), (1,)), ((), ())), precision=HIGH,
                           preferred_element_type=jnp.float32)


def _chol_inv(block):
    lower = jnp.linalg.cholesky(block, symmetrize_input=False)
    eye = jnp.eye(block.shape[0], dtype=block.dtype)
    inverse = lax.linalg.triangular_solve(lower, eye, left_side=True, lower=True)
    return lower, inverse


def _leaf_kernel(a_ref, w_ref, s_ref):
    n = a_ref.shape[0]
    s_ref[...] = a_ref[...]
    sub = lax.broadcasted_iota(jnp.int32, (n, n), 0)
    lane = lax.broadcasted_iota(jnp.int32, (n, n), 1)
    w_ref[...] = jnp.where(sub == lane, 1.0, 0.0).astype(jnp.float32)
    lane_row = lax.broadcasted_iota(jnp.int32, (1, n), 1)
    seg = 16
    for start in range(0, n, seg):
        rows = n - start
        lane_t = lax.broadcasted_iota(jnp.int32, (rows, n), 1)
        sub_col = lax.broadcasted_iota(jnp.int32, (rows, 1), 0) + start

        def step(j, carry, start=start, lane_t=lane_t, sub_col=sub_col):
            a = s_ref[start:, :]
            row = s_ref[pl.ds(j, 1), :]
            pivot = jnp.sum(jnp.where(lane_row == j, row, 0.0), axis=1, keepdims=True)
            inv_root = 1.0 / jnp.sqrt(pivot)
            col = jnp.sum(jnp.where(lane_t == j, a, 0.0), axis=1, keepdims=True)
            lcol = jnp.where(sub_col > j, col * inv_root, 0.0)
            lrow = jnp.where(lane_row >= j, row * inv_root, 0.0)
            s_ref[start:, :] = a - lcol * lrow
            wrow = w_ref[pl.ds(j, 1), :] * inv_root
            w_ref[start:, :] = w_ref[start:, :] - lcol * wrow
            w_ref[pl.ds(j, 1), :] = wrow
            return carry

        lax.fori_loop(start, start + seg, step, 0)

def _chol_inverse(block):
    n = block.shape[0]
    return pl.pallas_call(
        _leaf_kernel,
        out_shape=jax.ShapeDtypeStruct((n, n), jnp.float32),
        in_specs=[pl.BlockSpec(memory_space=pltpu.VMEM)],
        out_specs=pl.BlockSpec(memory_space=pltpu.VMEM),
        scratch_shapes=[pltpu.VMEM((n, n), jnp.float32)],
        cost_estimate=pl.CostEstimate(flops=6 * n * n * n, bytes_accessed=8 * n * n,
                                      transcendentals=n),
    )(block)


def precondition_blocks(blocks, nb, total_rows):
    block = blocks.shape[-1]
    na = nb - 1
    index = {p: k for k, p in enumerate(_tri_pairs(nb))}
    scale = 1.0 / total_rows
    flat = blocks.reshape(-1, block)
    panels = []
    for j in range(na):
        start = index[(j, j)] * block
        panel = flat[start:start + (nb - j) * block]
        panels.append(jnp.pad(panel, ((j * block, 0), (0, 0))))
    work = jnp.concatenate(panels, axis=1) * scale
    eye = jnp.eye(block, dtype=blocks.dtype)
    grad_factor = blocks[index[(na, na)]] * scale + damping * eye
    inverses = []
    for k in range(na):
        lo = k * block
        hi = lo + block
        diag = work[lo:hi, lo:hi] + damping * eye
        inverse = _chol_inverse(diag)
        inverses.append(inverse)
        panel = _mm_nt(work[hi:, lo:hi], inverse)
        work = work.at[hi:, lo:hi].set(panel)
        if k + 1 < na:
            update = _mm_nt(panel, panel[: (na - k - 1) * block])
            work = work.at[hi:, hi:].add(-update)
    solved_t = work[na * block:, :]
    pieces = [None] * na
    for k in reversed(range(na)):
        lo = k * block
        hi = lo + block
        rhs = solved_t[:, lo:hi].T
        if k + 1 < na:
            below = jnp.concatenate(pieces[k + 1:], axis=0)
            rhs = rhs - _mm_t(work[hi:na * block, lo:hi], below)
        pieces[k] = _mm_t(inverses[k], rhs)
    left_solved = jnp.concatenate(pieces, axis=0)
    grad_inverse = _chol_inverse(grad_factor)
    return _mm(_mm_nt(left_solved, grad_inverse), grad_inverse)


def body(line_columns, line_widths, layer_owner):
    layer_count, positions, packed_width = line_columns.shape
    channels = packed_width // 4
    full_width = 10 * channels
    n_replicas = 1
    for axis in DP_AXES:
        n_replicas = n_replicas * lax.axis_size(axis)
    n_owners = lax.axis_size(OWNER_AXES[0]) * lax.axis_size(OWNER_AXES[1])
    per_owner = layer_count // n_owners
    total_rows = n_replicas * n_owners * positions
    ordered = jnp.take(line_columns, layer_owner, axis=0, mode="clip")
    width_copies = jnp.broadcast_to(line_widths[None, :, :], (n_owners, 1, line_widths.shape[1]))
    source_widths = lax.all_to_all(width_copies, OWNER_AXES, split_axis=0, concat_axis=1, tiled=True)
    source_widths = source_widths.reshape(n_owners, line_widths.shape[1])
    me = lax.axis_index(OWNER_AXES)
    pieces = [lax.dynamic_index_in_dim(ordered, me, 0, keepdims=False)]
    piece_widths = [lax.dynamic_index_in_dim(source_widths, me, 0, keepdims=False)]
    for k in range(1, n_owners):
        outgoing = lax.dynamic_index_in_dim(ordered, (me + k) % n_owners, 0, keepdims=False)
        perm = [(o, (o + k) % n_owners) for o in range(n_owners)]
        pieces.append(lax.ppermute(outgoing, OWNER_AXES, perm))
        piece_widths.append(
            lax.dynamic_index_in_dim(source_widths, (me - k) % n_owners, 0, keepdims=False))
    blocks = jnp.stack(pieces)[None]
    columns = patch_columns(blocks, jnp.stack(piece_widths))
    columns = columns.reshape(n_owners * positions, full_width)
    block = 128
    nb = full_width // block
    n_blocks = nb * (nb + 1) // 2
    padded = -(-n_blocks * block // (8 * n_replicas)) * 8 * n_replicas // block
    panels = [
        lax.dot_general(columns[:, j * block:], columns[:, j * block:(j + 1) * block],
                        (((0,), (0,)), ((), ())), preferred_element_type=jnp.float32)
        for j in range(nb)
    ]
    panels.append(jnp.zeros(((padded - n_blocks) * block, block), jnp.float32))
    mine = jnp.concatenate(panels, axis=0)
    for axis in SCATTER_ORDER:
        mine = lax.psum_scatter(mine, axis, scatter_dimension=0, tiled=True)
    gathered = mine
    for axis in SCATTER_ORDER[::-1]:
        gathered = lax.all_gather(gathered, axis, axis=0, tiled=True)
    gathered = gathered.reshape(padded, block, block)
    results = precondition_blocks(gathered, nb, total_rows)[None]
    return lax.all_gather(results, OWNER_AXES, axis=0, tiled=True)


DP_AXES = ("dp_x", "dp_z", "dp_y")
SCATTER_ORDER = ("dp_y", "dp_x", "dp_z")


OWNER_AXES = ("owner_z", "owner_c")


def solution(mesh):
    dp_shape = (4, 2, mesh.shape["dp"] // 8)
    owner_shape = (mesh.shape["owner"] // 2, 2)
    devices = mesh.devices.reshape(dp_shape + owner_shape)
    fine = jax.sharding.Mesh(devices, DP_AXES + OWNER_AXES)
    rows = DP_AXES + OWNER_AXES
    in_specs = (P(None, rows, None), P(rows, None), P())
    out_specs = P()
    return jax.shard_map(body, mesh=fine, in_specs=in_specs, out_specs=out_specs, check_vma=False)
```

```python
import numpy as np
import jax
import jax.numpy as jnp
from jax import lax
from jax.experimental import pallas as pl
from jax.experimental.pallas import tpu as pltpu
from jax.sharding import PartitionSpec as P

damping = 0.1


def patch_columns(block, widths):
    positions = block.shape[-2]
    channels = block.shape[-1] // 4
    line_ends = jnp.cumsum(widths, axis=-1).astype(jnp.int32)
    line_starts = line_ends - widths
    place = jnp.arange(positions, dtype=jnp.int32)[:, None]
    opening = jnp.any(place == line_starts[..., None, :], axis=-1)[..., None]
    closing = jnp.any(place + 1 == line_ends[..., None, :], axis=-1)[..., None]
    inside = place < line_ends[..., None, -1:]
    features = block[..., : 3 * channels]
    gradients = block[..., 3 * channels :]
    padding = jnp.zeros_like(features[..., :1, :])
    before = jnp.concatenate([padding, features[..., :-1, :]], axis=-2)
    after = jnp.concatenate([features[..., 1:, :], padding], axis=-2)
    before = jnp.where(opening, jnp.zeros_like(before), before)
    after = jnp.where(closing, jnp.zeros_like(after), after)
    stacked = jnp.concatenate([before, features, after, gradients], axis=-1)
    return jnp.where(inside, stacked, jnp.zeros_like(stacked))


def precondition(factor, total_rows):
    full_width = factor.shape[0]
    patch_width = full_width // 10 * 9
    scaled = factor / total_rows
    act_factor = scaled[:patch_width, :patch_width] + damping * jnp.eye(
        patch_width, dtype=factor.dtype
    )
    grad_factor = scaled[patch_width:, patch_width:] + damping * jnp.eye(
        full_width - patch_width, dtype=factor.dtype
    )
    cross_term = scaled[:patch_width, patch_width:]
    act_cholesky = jnp.linalg.cholesky(act_factor)
    left_solved = jax.scipy.linalg.cho_solve((act_cholesky, True), cross_term)
    grad_cholesky = jnp.linalg.cholesky(grad_factor)
    return jax.scipy.linalg.cho_solve((grad_cholesky, True), left_solved.T).T


def _tri_pairs(nb):
    return [(i, j) for j in range(nb) for i in range(j, nb)]


def pack_lower(gram, block):
    nb = gram.shape[0] // block
    tiles = gram.reshape(nb, block, nb, block).transpose(0, 2, 1, 3)
    pairs = _tri_pairs(nb)
    rows = np.array([p[0] for p in pairs], dtype=np.int32)
    cols = np.array([p[1] for p in pairs], dtype=np.int32)
    return tiles[rows, cols]


def unpack_lower(blocks, nb):
    block = blocks.shape[-1]
    index = {p: k for k, p in enumerate(_tri_pairs(nb))}
    pick = np.array([[index[(max(i, j), min(i, j))] for j in range(nb)] for i in range(nb)], dtype=np.int32)
    upper = np.array([[i < j for j in range(nb)] for i in range(nb)])
    tiles = blocks[pick]
    tiles = jnp.where(upper[:, :, None, None], jnp.swapaxes(tiles, -1, -2), tiles)
    return tiles.transpose(0, 2, 1, 3).reshape(nb * block, nb * block)


HIGH = lax.Precision.HIGHEST


def _mm(a, b):
    return jnp.dot(a, b, precision=HIGH, preferred_element_type=jnp.float32)


def _mm_t(a, b):
    return lax.dot_general(a, b, (((0,), (0,)), ((), ())), precision=HIGH,
                           preferred_element_type=jnp.float32)


def _mm_nt(a, b):
    return lax.dot_general(a, b, (((1,), (1,)), ((), ())), precision=HIGH,
                           preferred_element_type=jnp.float32)


def _chol_inv(block):
    lower = jnp.linalg.cholesky(block, symmetrize_input=False)
    eye = jnp.eye(block.shape[0], dtype=block.dtype)
    inverse = lax.linalg.triangular_solve(lower, eye, left_side=True, lower=True)
    return lower, inverse


def _leaf_kernel(a_ref, w_ref, s_ref):
    count, n, _ = a_ref.shape
    s_ref[...] = a_ref[...]
    sub = lax.broadcasted_iota(jnp.int32, (n, n), 0)
    lane = lax.broadcasted_iota(jnp.int32, (n, n), 1)
    eye = jnp.where(sub == lane, 1.0, 0.0).astype(jnp.float32)
    for m in range(count):
        w_ref[m] = eye
    lane_row = lax.broadcasted_iota(jnp.int32, (1, n), 1)
    seg = 16
    for start in range(0, n, seg):
        rows = n - start
        lane_t = lax.broadcasted_iota(jnp.int32, (rows, n), 1)
        sub_col = lax.broadcasted_iota(jnp.int32, (rows, 1), 0) + start

        def step(j, carry, start=start, lane_t=lane_t, sub_col=sub_col):
            for m in range(count):
                a = s_ref[m, start:, :]
                row = s_ref[m, pl.ds(j, 1), :]
                pivot = jnp.sum(jnp.where(lane_row == j, row, 0.0), axis=1, keepdims=True)
                inv_root = 1.0 / jnp.sqrt(pivot)
                col = jnp.sum(jnp.where(lane_t == j, a, 0.0), axis=1, keepdims=True)
                lcol = jnp.where(sub_col > j, col * inv_root, 0.0)
                lrow = jnp.where(lane_row >= j, row * inv_root, 0.0)
                s_ref[m, start:, :] = a - lcol * lrow
                wrow = w_ref[m, pl.ds(j, 1), :] * inv_root
                w_ref[m, start:, :] = w_ref[m, start:, :] - lcol * wrow
                w_ref[m, pl.ds(j, 1), :] = wrow
            return carry

        lax.fori_loop(start, start + seg, step, 0)


def _chol_inverse(*blocks):
    stacked = jnp.stack(blocks)
    count, n, _ = stacked.shape
    out = pl.pallas_call(
        _leaf_kernel,
        out_shape=jax.ShapeDtypeStruct((count, n, n), jnp.float32),
        in_specs=[pl.BlockSpec(memory_space=pltpu.VMEM)],
        out_specs=pl.BlockSpec(memory_space=pltpu.VMEM),
        scratch_shapes=[pltpu.VMEM((count, n, n), jnp.float32)],
        cost_estimate=pl.CostEstimate(flops=6 * count * n * n * n, bytes_accessed=8 * count * n * n,
                                      transcendentals=count * n),
    )(stacked)
    return [out[m] for m in range(count)]

def precondition_blocks(blocks, nb, total_rows):
    block = blocks.shape[-1]
    na = nb - 1
    index = {p: k for k, p in enumerate(_tri_pairs(nb))}
    scale = 1.0 / total_rows
    flat = blocks.reshape(-1, block)
    panels = []
    for j in range(na):
        start = index[(j, j)] * block
        panel = flat[start:start + (nb - j) * block]
        panels.append(jnp.pad(panel, ((j * block, 0), (0, 0))))
    work = jnp.concatenate(panels, axis=1) * scale
    eye = jnp.eye(block, dtype=blocks.dtype)
    grad_factor = blocks[index[(na, na)]] * scale + damping * eye
    inverses = []
    for k in range(na):
        lo = k * block
        hi = lo + block
        diag = work[lo:hi, lo:hi] + damping * eye
        if k == 0:
            inverse, grad_inverse = _chol_inverse(diag, grad_factor)
        else:
            (inverse,) = _chol_inverse(diag)
        inverses.append(inverse)
        panel = _mm_nt(work[hi:, lo:hi], inverse)
        work = work.at[hi:, lo:hi].set(panel)
        if k + 1 < na:
            update = _mm_nt(panel, panel[: (na - k - 1) * block])
            work = work.at[hi:, hi:].add(-update)
    solved_t = work[na * block:, :]
    pieces = [None] * na
    for k in reversed(range(na)):
        lo = k * block
        hi = lo + block
        rhs = solved_t[:, lo:hi].T
        if k + 1 < na:
            below = jnp.concatenate(pieces[k + 1:], axis=0)
            rhs = rhs - _mm_t(work[hi:na * block, lo:hi], below)
        pieces[k] = _mm_t(inverses[k], rhs)
    left_solved = jnp.concatenate(pieces, axis=0)
    return _mm(_mm_nt(left_solved, grad_inverse), grad_inverse)


def body(line_columns, line_widths, layer_owner):
    layer_count, positions, packed_width = line_columns.shape
    channels = packed_width // 4
    full_width = 10 * channels
    n_replicas = 1
    for axis in DP_AXES:
        n_replicas = n_replicas * lax.axis_size(axis)
    n_owners = lax.axis_size(OWNER_AXES[0]) * lax.axis_size(OWNER_AXES[1])
    per_owner = layer_count // n_owners
    total_rows = n_replicas * n_owners * positions
    ordered = jnp.take(line_columns, layer_owner, axis=0, mode="clip")
    width_copies = jnp.broadcast_to(line_widths[None, :, :], (n_owners, 1, line_widths.shape[1]))
    received, source_widths = (
        lax.all_to_all(ordered, OWNER_AXES, split_axis=0, concat_axis=1, tiled=True),
        lax.all_to_all(width_copies, OWNER_AXES, split_axis=0, concat_axis=1, tiled=True),
    )
    blocks = received.reshape(per_owner, n_owners, positions, packed_width)
    columns = patch_columns(blocks, source_widths.reshape(n_owners, line_widths.shape[1]))
    columns = columns.reshape(n_owners * positions, full_width)
    block = 128
    nb = full_width // block
    n_blocks = nb * (nb + 1) // 2
    padded = -(-n_blocks * block // (8 * n_replicas)) * 8 * n_replicas // block
    panels = [
        lax.dot_general(columns[:, j * block:], columns[:, j * block:(j + 1) * block],
                        (((0,), (0,)), ((), ())), preferred_element_type=jnp.float32)
        for j in range(nb)
    ]
    panels.append(jnp.zeros(((padded - n_blocks) * block, block), jnp.float32))
    mine = jnp.concatenate(panels, axis=0)
    for axis in SCATTER_ORDER:
        mine = lax.psum_scatter(mine, axis, scatter_dimension=0, tiled=True)
    gathered = mine
    for axis in SCATTER_ORDER[::-1]:
        gathered = lax.all_gather(gathered, axis, axis=0, tiled=True)
    gathered = gathered.reshape(padded, block, block)
    results = precondition_blocks(gathered, nb, total_rows)[None]
    return lax.all_gather(results, OWNER_AXES, axis=0, tiled=True)


DP_AXES = ("dp_x", "dp_z", "dp_y")
SCATTER_ORDER = ("dp_y", "dp_x", "dp_z")


OWNER_AXES = ("owner_z", "owner_c")


def solution(mesh):
    dp_shape = (4, 2, mesh.shape["dp"] // 8)
    owner_shape = (mesh.shape["owner"] // 2, 2)
    devices = mesh.devices.reshape(dp_shape + owner_shape)
    fine = jax.sharding.Mesh(devices, DP_AXES + OWNER_AXES)
    rows = DP_AXES + OWNER_AXES
    in_specs = (P(None, rows, None), P(rows, None), P())
    out_specs = P()
    return jax.shard_map(body, mesh=fine, in_specs=in_specs, out_specs=out_specs, check_vma=False)
```

```python
import numpy as np
import jax
import jax.numpy as jnp
from jax import lax
from jax.experimental import pallas as pl
from jax.experimental.pallas import tpu as pltpu
from jax.sharding import PartitionSpec as P

damping = 0.1


def patch_columns(block, widths):
    positions = block.shape[-2]
    channels = block.shape[-1] // 4
    line_ends = jnp.cumsum(widths, axis=-1).astype(jnp.int32)
    line_starts = line_ends - widths
    place = jnp.arange(positions, dtype=jnp.int32)[:, None]
    opening = jnp.any(place == line_starts[..., None, :], axis=-1)[..., None]
    closing = jnp.any(place + 1 == line_ends[..., None, :], axis=-1)[..., None]
    inside = place < line_ends[..., None, -1:]
    features = block[..., : 3 * channels]
    gradients = block[..., 3 * channels :]
    padding = jnp.zeros_like(features[..., :1, :])
    before = jnp.concatenate([padding, features[..., :-1, :]], axis=-2)
    after = jnp.concatenate([features[..., 1:, :], padding], axis=-2)
    before = jnp.where(opening, jnp.zeros_like(before), before)
    after = jnp.where(closing, jnp.zeros_like(after), after)
    stacked = jnp.concatenate([before, features, after, gradients], axis=-1)
    return jnp.where(inside, stacked, jnp.zeros_like(stacked))


def precondition(factor, total_rows):
    full_width = factor.shape[0]
    patch_width = full_width // 10 * 9
    scaled = factor / total_rows
    act_factor = scaled[:patch_width, :patch_width] + damping * jnp.eye(
        patch_width, dtype=factor.dtype
    )
    grad_factor = scaled[patch_width:, patch_width:] + damping * jnp.eye(
        full_width - patch_width, dtype=factor.dtype
    )
    cross_term = scaled[:patch_width, patch_width:]
    act_cholesky = jnp.linalg.cholesky(act_factor)
    left_solved = jax.scipy.linalg.cho_solve((act_cholesky, True), cross_term)
    grad_cholesky = jnp.linalg.cholesky(grad_factor)
    return jax.scipy.linalg.cho_solve((grad_cholesky, True), left_solved.T).T


def _tri_pairs(nb):
    return [(i, j) for j in range(nb) for i in range(j, nb)]


def pack_lower(gram, block):
    nb = gram.shape[0] // block
    tiles = gram.reshape(nb, block, nb, block).transpose(0, 2, 1, 3)
    pairs = _tri_pairs(nb)
    rows = np.array([p[0] for p in pairs], dtype=np.int32)
    cols = np.array([p[1] for p in pairs], dtype=np.int32)
    return tiles[rows, cols]


def unpack_lower(blocks, nb):
    block = blocks.shape[-1]
    index = {p: k for k, p in enumerate(_tri_pairs(nb))}
    pick = np.array([[index[(max(i, j), min(i, j))] for j in range(nb)] for i in range(nb)], dtype=np.int32)
    upper = np.array([[i < j for j in range(nb)] for i in range(nb)])
    tiles = blocks[pick]
    tiles = jnp.where(upper[:, :, None, None], jnp.swapaxes(tiles, -1, -2), tiles)
    return tiles.transpose(0, 2, 1, 3).reshape(nb * block, nb * block)


HIGH = lax.Precision.HIGHEST


def _mm(a, b):
    return jnp.dot(a, b, precision=HIGH, preferred_element_type=jnp.float32)


def _mm_t(a, b):
    return lax.dot_general(a, b, (((0,), (0,)), ((), ())), precision=HIGH,
                           preferred_element_type=jnp.float32)


def _mm_nt(a, b):
    return lax.dot_general(a, b, (((1,), (1,)), ((), ())), precision=HIGH,
                           preferred_element_type=jnp.float32)


def _chol_inv(block):
    lower = jnp.linalg.cholesky(block, symmetrize_input=False)
    eye = jnp.eye(block.shape[0], dtype=block.dtype)
    inverse = lax.linalg.triangular_solve(lower, eye, left_side=True, lower=True)
    return lower, inverse


def _leaf_kernel(a_ref, w_ref, s_ref):
    n = a_ref.shape[0]
    s_ref[...] = a_ref[...]
    sub = lax.broadcasted_iota(jnp.int32, (n, n), 0)
    lane = lax.broadcasted_iota(jnp.int32, (n, n), 1)
    w_ref[...] = jnp.where(sub == lane, 1.0, 0.0).astype(jnp.float32)
    lane_row = lax.broadcasted_iota(jnp.int32, (1, n), 1)
    seg = 16
    for start in range(0, n, seg):
        rows = n - start
        lane_t = lax.broadcasted_iota(jnp.int32, (rows, n), 1)
        sub_col = lax.broadcasted_iota(jnp.int32, (rows, 1), 0) + start

        def step(j, carry, start=start, lane_t=lane_t, sub_col=sub_col):
            a = s_ref[start:, :]
            row = s_ref[pl.ds(j, 1), :]
            pivot = jnp.sum(jnp.where(lane_row == j, row, 0.0), axis=1, keepdims=True)
            inv_root = 1.0 / jnp.sqrt(pivot)
            col = jnp.sum(jnp.where(lane_t == j, a, 0.0), axis=1, keepdims=True)
            lcol = jnp.where(sub_col > j, col * inv_root, 0.0)
            lrow = jnp.where(lane_row >= j, row * inv_root, 0.0)
            s_ref[start:, :] = a - lcol * lrow
            wrow = w_ref[pl.ds(j, 1), :] * inv_root
            w_ref[start:, :] = w_ref[start:, :] - lcol * wrow
            w_ref[pl.ds(j, 1), :] = wrow
            return carry

        lax.fori_loop(start, start + seg, step, 0)

def _chol_inverse(block):
    n = block.shape[0]
    return pl.pallas_call(
        _leaf_kernel,
        out_shape=jax.ShapeDtypeStruct((n, n), jnp.float32),
        in_specs=[pl.BlockSpec(memory_space=pltpu.VMEM)],
        out_specs=pl.BlockSpec(memory_space=pltpu.VMEM),
        scratch_shapes=[pltpu.VMEM((n, n), jnp.float32)],
        cost_estimate=pl.CostEstimate(flops=6 * n * n * n, bytes_accessed=8 * n * n,
                                      transcendentals=n),
    )(block)


def precondition_blocks(blocks, nb, total_rows):
    block = blocks.shape[-1]
    na = nb - 1
    index = {p: k for k, p in enumerate(_tri_pairs(nb))}
    scale = 1.0 / total_rows
    flat = blocks.reshape(-1, block)
    panels = []
    for j in range(na):
        start = index[(j, j)] * block
        panel = flat[start:start + (nb - j) * block]
        panels.append(jnp.pad(panel, ((j * block, 0), (0, 0))))
    work = jnp.concatenate(panels, axis=1) * scale
    eye = jnp.eye(block, dtype=blocks.dtype)
    grad_factor = blocks[index[(na, na)]] * scale + damping * eye
    inverses = []
    for k in range(na):
        lo = k * block
        hi = lo + block
        diag = work[lo:hi, lo:hi] + damping * eye
        inverse = _chol_inverse(diag)
        inverses.append(inverse)
        panel = _mm_nt(work[hi:, lo:hi], inverse)
        work = work.at[hi:, lo:hi].set(panel)
        if k + 1 < na:
            update = _mm_nt(panel, panel[: (na - k - 1) * block])
            work = work.at[hi:, hi:].add(-update)
    solved_t = work[na * block:, :]
    left_solved = jnp.zeros((na * block, block), jnp.float32)
    for k in reversed(range(na)):
        lo = k * block
        hi = lo + block
        rhs = solved_t[:, lo:hi].T
        if k + 1 < na:
            rhs = rhs - _mm_t(work[hi:na * block, lo:hi], left_solved[hi:])
        left_solved = left_solved.at[lo:hi].set(_mm_t(inverses[k], rhs))
    grad_inverse = _chol_inverse(grad_factor)
    return _mm(_mm_nt(left_solved, grad_inverse), grad_inverse)


def body(line_columns, line_widths, layer_owner):
    layer_count, positions, packed_width = line_columns.shape
    channels = packed_width // 4
    full_width = 10 * channels
    n_replicas = 1
    for axis in DP_AXES:
        n_replicas = n_replicas * lax.axis_size(axis)
    n_owners = lax.axis_size(OWNER_AXES[0]) * lax.axis_size(OWNER_AXES[1])
    per_owner = layer_count // n_owners
    total_rows = n_replicas * n_owners * positions
    ordered = jnp.take(line_columns, layer_owner, axis=0, mode="clip")
    width_copies = jnp.broadcast_to(line_widths[None, :, :], (n_owners, 1, line_widths.shape[1]))
    received, source_widths = (
        lax.all_to_all(ordered, OWNER_AXES, split_axis=0, concat_axis=1, tiled=True),
        lax.all_to_all(width_copies, OWNER_AXES, split_axis=0, concat_axis=1, tiled=True),
    )
    blocks = received.reshape(per_owner, n_owners, positions, packed_width)
    columns = patch_columns(blocks, source_widths.reshape(n_owners, line_widths.shape[1]))
    columns = columns.reshape(n_owners * positions, full_width)
    block = 128
    nb = full_width // block
    n_blocks = nb * (nb + 1) // 2
    padded = -(-n_blocks * block // (8 * n_replicas)) * 8 * n_replicas // block
    panels = [
        lax.dot_general(columns[:, j * block:], columns[:, j * block:(j + 1) * block],
                        (((0,), (0,)), ((), ())), preferred_element_type=jnp.float32)
        for j in range(nb)
    ]
    panels.append(jnp.zeros(((padded - n_blocks) * block, block), jnp.float32))
    mine = jnp.concatenate(panels, axis=0)
    for axis in SCATTER_ORDER:
        mine = lax.psum_scatter(mine, axis, scatter_dimension=0, tiled=True)
    gathered = mine
    for axis in SCATTER_ORDER[::-1]:
        gathered = lax.all_gather(gathered, axis, axis=0, tiled=True)
    gathered = gathered.reshape(padded, block, block)
    results = precondition_blocks(gathered, nb, total_rows)[None]
    return lax.all_gather(results, OWNER_AXES, axis=0, tiled=True)


DP_AXES = ("dp_x", "dp_z", "dp_y")
SCATTER_ORDER = ("dp_y", "dp_x", "dp_z")


OWNER_AXES = ("owner_z", "owner_c")


def solution(mesh):
    dp_shape = (4, 2, mesh.shape["dp"] // 8)
    owner_shape = (mesh.shape["owner"] // 2, 2)
    devices = mesh.devices.reshape(dp_shape + owner_shape)
    fine = jax.sharding.Mesh(devices, DP_AXES + OWNER_AXES)
    rows = DP_AXES + OWNER_AXES
    in_specs = (P(None, rows, None), P(rows, None), P())
    out_specs = P()
    return jax.shard_map(body, mesh=fine, in_specs=in_specs, out_specs=out_specs, check_vma=False)
```
